256 devices in a mesh: row: 8 (over z_lo, y), col: 32 (over z_hi, x, core).
Axes of the slice: x: 4, y: 4, z: 8 (z_hi: 4, z_lo: 2; z = z_hi * 2 + z_lo), core: 2. Of those that a mesh axis runs over, the one named last changes fastest.
Arguments:
- strip: float32 [12, 2048, 2, 1024], P(None, 'col', None, 'row'), may hold values from -6 to 6
- lower: float32 [12, 2048, 2, 1024], P(None, 'col', None, 'row'), may hold values from -1.6 to 1.6, as said below
Outputs:
- reduced: float32 [12, 2048, 2, 1024], P(None, 'col', None, 'row')
The draws below stay inside these ranges and needn't reach their ends.
Inputs may be any that keep to these rules, and one draw needn't show every extreme that they name: `lower`: in the first 2048 rows the diagonal lies between 0.8 and 1.6 and entries above it are zero.
All inputs are finite; a program needn't handle non-finite values.
Results may differ from the reference program's by a relative error of at most 0.00013.
Values sent between devices are 32-bit elements; how exact they have to be, the bound alone decides.
No kernel may reach another device: no remote copies, remote signals or barrier semaphores. Data moves between devices by JAX's collectives and lax.ppermute only.
A program may use at most 64 MiB of HBM per device.

```python
import math
import jax
import jax.numpy as jnp
from jax import lax

NB = 1024
ROUNDS = 12


def draw_lower(key, part):
    key_main, key_diag = jax.random.split(key)
    shape = (ROUNDS, 2 * NB, 2, NB)
    noise = jnp.clip(jax.random.normal(key_main, shape, jnp.float32), -6.0, 6.0)
    diag_values = jax.random.uniform(key_diag, shape, jnp.float32, 0.8, 1.6)
    row_index = lax.broadcasted_iota(jnp.int32, shape, 0) * (2 * NB) + lax.broadcasted_iota(jnp.int32, shape, 1)
    col_block = lax.broadcasted_iota(jnp.int32, shape, 2)
    col_inner = lax.broadcasted_iota(jnp.int32, shape, 3)
    row_block = row_index // NB
    row_inner = row_index % NB
    in_lead = row_index < 2 * NB
    strict_lower = jnp.where(col_inner < row_inner, 0.6 / math.sqrt(NB) * noise, 0.0)
    diag_part = jnp.where(col_inner == row_inner, diag_values, strict_lower)
    cross_value = 0.8 / math.sqrt(NB) * noise
    lead_value = jnp.where(row_block == col_block, diag_part, jnp.where(row_block > col_block, cross_value, 0.0))
    trail_value = noise / math.sqrt(2 * NB)
    return jnp.where(in_lead, lead_value, trail_value)


def block_levels(stream_key, dims, pieces, smallest, largest):
    factor_of = 1.0
    for dim, blocks in pieces:
        heights = jax.random.uniform(jax.random.fold_in(jax.random.fold_in(stream_key, 6), dim), (blocks,), jnp.float32, smallest / len(pieces), largest / len(pieces))
        factor_of = factor_of * jnp.repeat(jnp.exp(heights), dims[dim] // blocks).reshape((-1,) + (1,) * (len(dims) - 1 - dim))
    return factor_of


def bell_draw(rng, shape, spread, reach, cuts=(), dtype=jnp.bfloat16):
    factor_of = block_levels(rng, shape, cuts, -0.22, 0.18) if cuts else 1.0
    values = jax.random.normal(rng, shape, jnp.float32) * spread * factor_of
    return jnp.minimum(jnp.maximum(values, -reach), reach).astype(dtype)


def setup_inputs(seed: int = 0) -> dict:
    keys = jax.random.split(jax.random.key(seed), 3)
    return {
        "strip": bell_draw(keys[0], (ROUNDS, 2 * NB, 2, NB), 1.0, 6.0, ((1, 32), (3, 8)), jnp.float32),
        "lower": draw_lower(jax.random.fold_in(keys[2], 71), 0),
    }


highest = lax.Precision.HIGHEST


def multiply_full(left_side, right_side):
    return jnp.dot(left_side, right_side, precision=highest, preferred_element_type=jnp.float32)


def reference(strip, lower):
    full_strip = strip.reshape(ROUNDS * 2 * NB, 2 * NB)
    factors = lower.reshape(ROUNDS * 2 * NB, 2 * NB)
    first_inverse = factors[:NB, :NB]
    cross_part = factors[NB:2 * NB, :NB]
    second_inverse = factors[NB:2 * NB, NB:2 * NB]
    below_part = factors[2 * NB:, :]
    upper_half = multiply_full(first_inverse, full_strip[:, :NB].T)
    remainder = full_strip[:, NB:].T - multiply_full(cross_part, upper_half)
    lower_half = multiply_full(second_inverse, remainder)
    solved = jnp.concatenate([upper_half.T, lower_half.T], axis=1)
    lead_rows = solved[:2 * NB]
    lead_first = multiply_full(first_inverse, lead_rows[:NB])
    lead_second = multiply_full(second_inverse, lead_rows[NB:] - multiply_full(cross_part, lead_first))
    lead_block = jnp.concatenate([lead_first, lead_second], axis=0)
    trail_rows = solved[2 * NB:] - multiply_full(below_part, lead_block)
    return jnp.concatenate([lead_block, trail_rows], axis=0).reshape(ROUNDS, 2 * NB, 2, NB)
```

```python
import jax
import jax.numpy as jnp
from jax import lax
from jax.sharding import PartitionSpec as P

highest = lax.Precision.HIGHEST


def times_rows(coeff, right_side):
    return jnp.dot(coeff, right_side, precision=highest, preferred_element_type=jnp.float32)


def times_rows_turned(coeff, right_turned):
    return lax.dot_general(
        coeff,
        right_turned,
        (((1,), (1,)), ((), ())),
        precision=highest,
        preferred_element_type=jnp.float32,
    )


def local(strip, lower):
    rounds = strip.shape[0]
    strip_width = strip.shape[1]
    row_run = strip.shape[3]
    row_count = lax.axis_size("row")
    col_count = lax.axis_size("col")
    block_size = row_run * row_count
    cols_here = rounds * strip_width
    trail_count = cols_here - strip_width
    share = block_size // col_count
    local_strip = strip.reshape(cols_here, 2, row_run)
    left_part = local_strip[:, 0, :]
    right_part = local_strip[:, 1, :]
    gathered = lax.all_gather(lower[0], "col", axis=0, tiled=True)
    first_cols = gathered[:block_size, 0, :]
    cross_cols = gathered[block_size:, 0, :]
    second_cols = gathered[block_size:, 1, :]

    col_position = lax.axis_index("col")
    start = col_position * share
    top_rows = lax.dynamic_slice_in_dim(gathered, start, share, 0)
    bottom_rows = lax.dynamic_slice_in_dim(gathered, block_size + start, share, 0)
    picked = jnp.concatenate([top_rows, bottom_rows], axis=0)
    picked_rows = lax.all_gather(picked, "row", axis=2, tiled=True)
    first_rows = picked_rows[:share, 0, :]
    cross_rows = picked_rows[share:, 0, :]
    second_rows = picked_rows[share:, 1, :]

    upper_half = lax.psum_scatter(
        times_rows_turned(first_cols, left_part), "row", scatter_dimension=0, tiled=True
    )
    carried = lax.psum_scatter(
        times_rows(cross_cols, upper_half), "row", scatter_dimension=0, tiled=True
    )
    remainder = right_part.T - carried
    lower_half = lax.psum_scatter(
        times_rows(second_cols, remainder), "row", scatter_dimension=0, tiled=True
    )
    solved = jnp.stack([upper_half.T, lower_half.T], axis=1)
    lead_rows = solved[:strip_width]
    tail_rows = solved[strip_width:].reshape(trail_count, 2 * row_run)

    lead_all = lax.all_gather(lead_rows, "col", axis=0, tiled=True)
    lead_all = lead_all.reshape(2 * block_size, 2 * row_run)
    first_piece = times_rows(first_rows, lead_all[:block_size])
    first_block = lax.all_gather(first_piece, "col", axis=0, tiled=True)
    lead_second = lax.dynamic_slice_in_dim(lead_all, block_size + start, share, 0)
    diff_piece = lead_second - times_rows(cross_rows, first_block)
    diff_block = lax.all_gather(diff_piece, "col", axis=0, tiled=True)
    second_piece = times_rows(second_rows, diff_block)
    second_block = lax.all_gather(second_piece, "col", axis=0, tiled=True)
    everything = jnp.concatenate([first_block, second_block], axis=0)
    solved_lead = lax.dynamic_slice_in_dim(everything, col_position * strip_width, strip_width, 0)

    left_rows = lower[1:].reshape(trail_count, 2 * row_run)
    grouped = everything.reshape(2, row_count, row_run, 2 * row_run).transpose(1, 0, 2, 3)
    swapped = lax.all_to_all(grouped, "row", split_axis=0, concat_axis=0, tiled=True)
    turned_block = swapped.reshape(row_count, 2, row_run, 2, row_run).transpose(0, 3, 4, 1, 2)
    turned_block = turned_block.reshape(row_count * 2 * row_run, 2 * row_run)
    summed = lax.psum_scatter(
        times_rows_turned(turned_block, left_rows), "row", scatter_dimension=0, tiled=True
    )
    update = summed.T
    reduced = jnp.concatenate([solved_lead, tail_rows - update], axis=0)
    return reduced.reshape(rounds, strip_width, 2, row_run)


def solution(mesh):
    in_specs = (P(None, "col", None, "row"), P(None, "col", None, "row"))
    out_specs = P(None, "col", None, "row")
    return jax.shard_map(local, mesh=mesh, in_specs=in_specs, out_specs=out_specs, check_vma=False)
```

```python
import jax
import jax.numpy as jnp
from jax import lax
from jax.sharding import PartitionSpec as P

highest = lax.Precision.HIGHEST


def times_rows(coeff, right_side):
    return jnp.dot(coeff, right_side, precision=highest, preferred_element_type=jnp.float32)


def times_rows_turned(coeff, right_turned):
    return lax.dot_general(
        coeff,
        right_turned,
        (((1,), (1,)), ((), ())),
        precision=highest,
        preferred_element_type=jnp.float32,
    )


def local(strip, lower):
    rounds = strip.shape[0]
    strip_width = strip.shape[1]
    row_run = strip.shape[3]
    row_count = lax.axis_size("row")
    col_count = lax.axis_size("col")
    block_size = row_run * row_count
    cols_here = rounds * strip_width
    trail_count = cols_here - strip_width
    share = block_size // col_count
    local_strip = strip.reshape(cols_here, 2, row_run)
    left_part = local_strip[:, 0, :]
    right_part = local_strip[:, 1, :]
    gathered = lax.all_gather(lower[0], "col", axis=0, tiled=True)
    first_cols = gathered[:block_size, 0, :]
    cross_cols = gathered[block_size:, 0, :]
    second_cols = gathered[block_size:, 1, :]

    col_position = lax.axis_index("col")
    start = col_position * share
    top_rows = lax.dynamic_slice_in_dim(gathered, start, share, 0)
    bottom_rows = lax.dynamic_slice_in_dim(gathered, block_size + start, share, 0)
    picked = jnp.concatenate([top_rows, bottom_rows], axis=0)
    picked_rows = lax.all_gather(picked, "row", axis=2, tiled=True)
    first_rows = picked_rows[:share, 0, :]
    second_rows = picked_rows[share:, 1, :]

    upper_half = lax.psum_scatter(
        times_rows_turned(first_cols, left_part), "row", scatter_dimension=0, tiled=True
    )
    carried = lax.psum_scatter(
        times_rows(cross_cols, upper_half), "row", scatter_dimension=0, tiled=True
    )
    remainder = right_part.T - carried
    lower_half = lax.psum_scatter(
        times_rows(second_cols, remainder), "row", scatter_dimension=0, tiled=True
    )
    solved = jnp.stack([upper_half.T, lower_half.T], axis=1)
    lead_rows = solved[:strip_width]
    tail_rows = solved[strip_width:].reshape(trail_count, 2 * row_run)

    cross_mix = lax.all_gather(times_rows(second_rows, cross_cols), "row", axis=1, tiled=True)
    chained = lax.all_gather(times_rows(cross_mix, first_cols), "row", axis=1, tiled=True)

    lead_all = lax.all_gather(lead_rows, "col", axis=0, tiled=True)
    lead_all = lead_all.reshape(2 * block_size, 2 * row_run)
    lead_first = lead_all[:block_size]
    first_piece = times_rows(first_rows, lead_first)
    second_piece = times_rows(second_rows, lead_all[block_size:]) - times_rows(chained, lead_first)
    pieces = jnp.concatenate([first_piece, second_piece], axis=0)
    everything = lax.all_gather(pieces, "col", axis=0, tiled=True)
    everything = everything.reshape(col_count, 2, share, 2 * row_run).transpose(1, 0, 2, 3)
    everything = everything.reshape(2 * block_size, 2 * row_run)
    solved_lead = lax.dynamic_slice_in_dim(everything, col_position * strip_width, strip_width, 0)

    left_rows = lower[1:].reshape(trail_count, 2 * row_run)
    grouped = everything.reshape(2, row_count, row_run, 2 * row_run).transpose(1, 0, 2, 3)
    swapped = lax.all_to_all(grouped, "row", split_axis=0, concat_axis=0, tiled=True)
    turned_block = swapped.reshape(row_count, 2, row_run, 2, row_run).transpose(0, 3, 4, 1, 2)
    turned_block = turned_block.reshape(row_count * 2 * row_run, 2 * row_run)
    summed = lax.psum_scatter(
        times_rows_turned(turned_block, left_rows), "row", scatter_dimension=0, tiled=True
    )
    update = summed.T
    reduced = jnp.concatenate([solved_lead, tail_rows - update], axis=0)
    return reduced.reshape(rounds, strip_width, 2, row_run)


def solution(mesh):
    in_specs = (P(None, "col", None, "row"), P(None, "col", None, "row"))
    out_specs = P(None, "col", None, "row")
    return jax.shard_map(local, mesh=mesh, in_specs=in_specs, out_specs=out_specs, check_vma=False)
```

```python
import jax
import jax.numpy as jnp
from jax import lax
from jax.sharding import PartitionSpec as P

highest = lax.Precision.HIGHEST


def times_rows(coeff, right_side):
    return jnp.dot(coeff, right_side, precision=highest, preferred_element_type=jnp.float32)


def times_rows_turned(coeff, right_turned):
    return lax.dot_general(
        coeff,
        right_turned,
        (((1,), (1,)), ((), ())),
        precision=highest,
        preferred_element_type=jnp.float32,
    )


def local(strip, lower):
    rounds = strip.shape[0]
    strip_width = strip.shape[1]
    row_run = strip.shape[3]
    row_count = lax.axis_size("row")
    col_count = lax.axis_size("col")
    block_size = row_run * row_count
    cols_here = rounds * strip_width
    share = block_size // col_count
    strip_rows = strip.reshape(cols_here, 2 * row_run)
    gathered = lax.all_gather(lower[0], "col", axis=0, tiled=True)
    first_cols = gathered[:block_size, 0, :]
    cross_cols = gathered[block_size:, 0, :]
    second_cols = gathered[block_size:, 1, :]

    col_position = lax.axis_index("col")
    start = col_position * share
    top_rows = lax.dynamic_slice_in_dim(gathered, start, share, 0)
    bottom_rows = lax.dynamic_slice_in_dim(gathered, block_size + start, share, 0)
    picked = jnp.concatenate([top_rows, bottom_rows], axis=0)
    picked_rows = lax.all_gather(picked, "row", axis=2, tiled=True)
    first_rows = picked_rows[:share, 0, :]
    second_rows = picked_rows[share:, 1, :]

    cross_mix = lax.all_gather(times_rows(second_rows, cross_cols), "row", axis=1, tiled=True)
    chained_piece = times_rows(cross_mix, first_cols)
    chained = lax.all_gather(chained_piece, "row", axis=1, tiled=True)
    chained_cols = lax.all_gather(chained_piece, "col", axis=0, tiled=True)

    inverse_cols = jnp.concatenate(
        [
            jnp.concatenate([first_cols, jnp.zeros_like(first_cols)], axis=1),
            jnp.concatenate([-chained_cols, second_cols], axis=1),
        ],
        axis=0,
    )
    inverse_cols = inverse_cols.reshape(2, row_count, row_run, 2 * row_run).transpose(1, 0, 2, 3)
    inverse_cols = inverse_cols.reshape(2 * block_size, 2 * row_run)
    lead_rows = lax.psum_scatter(
        times_rows_turned(inverse_cols, strip_rows[:strip_width]),
        "row",
        scatter_dimension=0,
        tiled=True,
    ).T

    lead_all = lax.all_gather(lead_rows, "col", axis=0, tiled=True)
    lead_first = lead_all[:block_size]
    first_piece = times_rows(first_rows, lead_first)
    second_piece = times_rows(second_rows, lead_all[block_size:]) - times_rows(chained, lead_first)
    pieces = jnp.concatenate([first_piece, second_piece], axis=0)
    everything = lax.all_gather(pieces, "col", axis=0, tiled=True)
    everything = everything.reshape(col_count, 2, share, 2 * row_run).transpose(1, 0, 2, 3)
    everything = everything.reshape(2 * block_size, 2 * row_run)
    solved_lead = lax.dynamic_slice_in_dim(everything, col_position * strip_width, strip_width, 0)

    left_rows = lower[1:].reshape(cols_here - strip_width, 2 * row_run)
    grouped = everything.reshape(2, row_count, row_run, 2 * row_run).transpose(1, 0, 2, 3)
    swapped = lax.all_to_all(grouped, "row", split_axis=0, concat_axis=0, tiled=True)
    turned_block = swapped.reshape(row_count, 2, row_run, 2, row_run).transpose(0, 3, 4, 1, 2)
    turned_block = turned_block.reshape(row_count * 2 * row_run, 2 * row_run)
    summed = lax.psum_scatter(
        times_rows_turned(inverse_cols, strip_rows[strip_width:])
        - times_rows_turned(turned_block, left_rows),
        "row",
        scatter_dimension=0,
        tiled=True,
    )
    reduced = jnp.concatenate([solved_lead, summed.T], axis=0)
    return reduced.reshape(rounds, strip_width, 2, row_run)


def solution(mesh):
    in_specs = (P(None, "col", None, "row"), P(None, "col", None, "row"))
    out_specs = P(None, "col", None, "row")
    return jax.shard_map(local, mesh=mesh, in_specs=in_specs, out_specs=out_specs, check_vma=False)
```

```python
import jax
import jax.numpy as jnp
from jax import lax
from jax.sharding import PartitionSpec as P

highest = lax.Precision.HIGHEST


def times_rows(coeff, right_side):
    return jnp.dot(coeff, right_side, precision=highest, preferred_element_type=jnp.float32)


def times_rows_turned(coeff, right_turned):
    return lax.dot_general(
        coeff,
        right_turned,
        (((1,), (1,)), ((), ())),
        precision=highest,
        preferred_element_type=jnp.float32,
    )


def local(strip, lower):
    rounds = strip.shape[0]
    strip_width = strip.shape[1]
    row_run = strip.shape[3]
    row_count = lax.axis_size("row")
    col_count = lax.axis_size("col")
    block_size = row_run * row_count
    cols_here = rounds * strip_width
    share = block_size // col_count
    strip_rows = strip.reshape(cols_here, 2 * row_run)
    gathered = lax.all_gather(lower[0], "col", axis=0, tiled=True)
    first_cols = gathered[:block_size, 0, :]
    cross_cols = gathered[block_size:, 0, :]
    second_cols = gathered[block_size:, 1, :]

    col_position = lax.axis_index("col")
    start = col_position * share
    top_rows = lax.dynamic_slice_in_dim(gathered, start, share, 0)
    bottom_rows = lax.dynamic_slice_in_dim(gathered, block_size + start, share, 0)
    picked = jnp.concatenate([top_rows, bottom_rows], axis=0)
    picked_rows = lax.all_gather(picked, "row", axis=2, tiled=True)
    first_rows = picked_rows[:share, 0, :]
    second_rows = picked_rows[share:, 1, :]

    cross_mix = lax.all_gather(times_rows(second_rows, cross_cols), "row", axis=1, tiled=True)
    chained_piece = times_rows(cross_mix, first_cols)
    chained = lax.all_gather(chained_piece, "row", axis=1, tiled=True)
    chained_cols = lax.all_gather(chained_piece, "col", axis=0, tiled=True)

    inverse_cols = jnp.concatenate(
        [
            jnp.concatenate([first_cols, jnp.zeros_like(first_cols)], axis=1),
            jnp.concatenate([-chained_cols, second_cols], axis=1),
        ],
        axis=0,
    )
    inverse_cols = inverse_cols.reshape(2, row_count, row_run, 2 * row_run).transpose(1, 0, 2, 3)
    inverse_cols = inverse_cols.reshape(2 * block_size, 2 * row_run)
    strip_lead = lax.all_gather(strip[0], "col", axis=0, tiled=True)
    strip_lead = strip_lead.reshape(2 * block_size, 2 * row_run)
    strip_first = strip_lead[:block_size]
    first_mixed = times_rows(first_rows, strip_first)
    second_mixed = times_rows(second_rows, strip_lead[block_size:]) - times_rows(chained, strip_first)
    mixed = jnp.concatenate([first_mixed, second_mixed], axis=0)
    pieces = lax.psum_scatter(
        times_rows_turned(inverse_cols, mixed), "row", scatter_dimension=0, tiled=True
    ).T
    everything = lax.all_gather(pieces, "col", axis=0, tiled=True)
    everything = everything.reshape(col_count, 2, share, 2 * row_run).transpose(1, 0, 2, 3)
    everything = everything.reshape(2 * block_size, 2 * row_run)
    solved_lead = lax.dynamic_slice_in_dim(everything, col_position * strip_width, strip_width, 0)

    left_rows = lower[1:].reshape(cols_here - strip_width, 2 * row_run)
    grouped = everything.reshape(2, row_count, row_run, 2 * row_run).transpose(1, 0, 2, 3)
    swapped = lax.all_to_all(grouped, "row", split_axis=0, concat_axis=0, tiled=True)
    turned_block = swapped.reshape(row_count, 2, row_run, 2, row_run).transpose(0, 3, 4, 1, 2)
    turned_block = turned_block.reshape(row_count * 2 * row_run, 2 * row_run)
    summed = lax.psum_scatter(
        times_rows_turned(inverse_cols, strip_rows[strip_width:])
        - times_rows_turned(turned_block, left_rows),
        "row",
        scatter_dimension=0,
        tiled=True,
    )
    reduced = jnp.concatenate([solved_lead, summed.T], axis=0)
    return reduced.reshape(rounds, strip_width, 2, row_run)


def solution(mesh):
    in_specs = (P(None, "col", None, "row"), P(None, "col", None, "row"))
    out_specs = P(None, "col", None, "row")
    return jax.shard_map(local, mesh=mesh, in_specs=in_specs, out_specs=out_specs, check_vma=False)
```

```python
import jax
import jax.numpy as jnp
from jax import lax
from jax.sharding import PartitionSpec as P

highest = lax.Precision.HIGHEST


def times_rows(coeff, right_side):
    return jnp.dot(coeff, right_side, precision=highest, preferred_element_type=jnp.float32)


def times_rows_turned(coeff, right_turned):
    return lax.dot_general(
        coeff,
        right_turned,
        (((1,), (1,)), ((), ())),
        precision=highest,
        preferred_element_type=jnp.float32,
    )


def local(strip, lower):
    rounds = strip.shape[0]
    strip_width = strip.shape[1]
    row_run = strip.shape[3]
    row_count = lax.axis_size("row")
    col_count = lax.axis_size("col")
    block_size = row_run * row_count
    cols_here = rounds * strip_width
    strip_rows = strip.reshape(cols_here, 2 * row_run)
    gathered = lax.all_gather(lower[0], "col", axis=0, tiled=True)
    first_cols = gathered[:block_size, 0, :]
    cross_cols = gathered[block_size:, 0, :]
    second_cols = gathered[block_size:, 1, :]

    col_position = lax.axis_index("col")
    lower_half = col_position * strip_width // block_size
    own_rows = lax.all_gather(lower[0], "row", axis=2, tiled=True)
    diag_rows = lax.dynamic_index_in_dim(own_rows, lower_half, 1, keepdims=False)
    below = lower_half == 1

    cross_mix = lax.all_gather(times_rows(own_rows[:, 1, :], cross_cols), "row", axis=1, tiled=True)
    chained_piece = times_rows(cross_mix, first_cols)
    chained = lax.all_gather(chained_piece, "row", axis=1, tiled=True)
    chained_cols = lax.all_gather(chained_piece, "col", axis=0, tiled=True)[block_size:]

    inverse_cols = jnp.concatenate(
        [
            jnp.concatenate([first_cols, jnp.zeros_like(first_cols)], axis=1),
            jnp.concatenate([-chained_cols, second_cols], axis=1),
        ],
        axis=0,
    )
    inverse_cols = inverse_cols.reshape(2, row_count, row_run, 2 * row_run).transpose(1, 0, 2, 3)
    inverse_cols = inverse_cols.reshape(2 * block_size, 2 * row_run)
    strip_lead = lax.all_gather(strip[0], "col", axis=0, tiled=True)
    strip_lead = strip_lead.reshape(2 * block_size, 2 * row_run)
    strip_first = strip_lead[:block_size]
    strip_diag = lax.dynamic_slice_in_dim(strip_lead, lower_half * block_size, block_size, 0)
    chained_term = jnp.where(below, times_rows(chained, strip_first), 0.0)
    mixed = times_rows(diag_rows, strip_diag) - chained_term
    solved_lead = lax.psum_scatter(
        times_rows_turned(inverse_cols, mixed), "row", scatter_dimension=0, tiled=True
    ).T
    everything = lax.all_gather(solved_lead, "col", axis=0, tiled=True)

    left_rows = lower[1:].reshape(cols_here - strip_width, 2 * row_run)
    grouped = everything.reshape(2, row_count, row_run, 2 * row_run).transpose(1, 0, 2, 3)
    swapped = lax.all_to_all(grouped, "row", split_axis=0, concat_axis=0, tiled=True)
    turned_block = swapped.reshape(row_count, 2, row_run, 2, row_run).transpose(0, 3, 4, 1, 2)
    turned_block = turned_block.reshape(row_count * 2 * row_run, 2 * row_run)
    summed = lax.psum_scatter(
        times_rows_turned(inverse_cols, strip_rows[strip_width:])
        - times_rows_turned(turned_block, left_rows),
        "row",
        scatter_dimension=0,
        tiled=True,
    )
    reduced = jnp.concatenate([solved_lead, summed.T], axis=0)
    return reduced.reshape(rounds, strip_width, 2, row_run)


def solution(mesh):
    in_specs = (P(None, "col", None, "row"), P(None, "col", None, "row"))
    out_specs = P(None, "col", None, "row")
    return jax.shard_map(local, mesh=mesh, in_specs=in_specs, out_specs=out_specs, check_vma=False)
```

```python
import jax
import jax.numpy as jnp
from jax import lax
from jax.sharding import PartitionSpec as P

highest = lax.Precision.HIGHEST


def times_rows(coeff, right_side):
    return jnp.dot(coeff, right_side, precision=highest, preferred_element_type=jnp.float32)


def times_rows_turned(coeff, right_turned):
    return lax.dot_general(
        coeff,
        right_turned,
        (((1,), (1,)), ((), ())),
        precision=highest,
        preferred_element_type=jnp.float32,
    )


def local(strip, lower):
    rounds = strip.shape[0]
    strip_width = strip.shape[1]
    row_run = strip.shape[3]
    row_count = lax.axis_size("row")
    col_count = lax.axis_size("col")
    block_size = row_run * row_count
    cols_here = rounds * strip_width
    strip_rows = strip.reshape(cols_here, 2 * row_run)
    gathered = lax.all_gather(lower[0], "col", axis=0, tiled=True)
    first_cols = gathered[:block_size, 0, :]
    cross_cols = gathered[block_size:, 0, :]
    second_cols = gathered[block_size:, 1, :]

    col_position = lax.axis_index("col")
    lower_half = col_position * strip_width // block_size
    own_rows = lax.all_gather(lower[0], "row", axis=2, tiled=True)
    diag_rows = lax.dynamic_index_in_dim(own_rows, lower_half, 1, keepdims=False)
    below = lower_half == 1

    cross_mix = lax.all_gather(times_rows(own_rows[:, 1, :], cross_cols), "row", axis=1, tiled=True)
    chained_piece = times_rows(cross_mix, first_cols)
    chained = lax.all_gather(chained_piece, "row", axis=1, tiled=True)
    chained_cols = lax.all_gather(chained_piece, "col", axis=0, tiled=True)[block_size:]

    inverse_cols = jnp.concatenate(
        [
            jnp.concatenate([first_cols, jnp.zeros_like(first_cols)], axis=1),
            jnp.concatenate([-chained_cols, second_cols], axis=1),
        ],
        axis=0,
    )
    inverse_cols = inverse_cols.reshape(2, row_count, row_run, 2 * row_run).transpose(1, 0, 2, 3)
    inverse_cols = inverse_cols.reshape(2 * block_size, 2 * row_run)
    strip_lead = lax.all_gather(strip[0], "col", axis=0, tiled=True)
    strip_lead = strip_lead.reshape(2 * block_size, 2 * row_run)
    strip_first = strip_lead[:block_size]
    strip_diag = lax.dynamic_slice_in_dim(strip_lead, lower_half * block_size, block_size, 0)
    chained_term = jnp.where(below, times_rows(chained, strip_first), 0.0)
    mixed = times_rows(diag_rows, strip_diag) - chained_term
    solved_lead = lax.psum_scatter(
        times_rows_turned(inverse_cols, mixed), "row", scatter_dimension=0, tiled=True
    ).T
    everything = lax.all_gather(solved_lead, "col", axis=0, tiled=True)

    trail_count = cols_here - strip_width
    copies = jnp.broadcast_to(lower[1:].reshape(1, trail_count, 2, row_run), (row_count, trail_count, 2, row_run))
    full_left = lax.all_to_all(copies, "row", split_axis=0, concat_axis=0, tiled=True)
    full_left = full_left.transpose(1, 2, 0, 3).reshape(trail_count, 2 * block_size)
    summed = lax.psum_scatter(
        times_rows_turned(inverse_cols, strip_rows[strip_width:]),
        "row",
        scatter_dimension=0,
        tiled=True,
    )
    tail_rows = summed.T - times_rows(full_left, everything)
    reduced = jnp.concatenate([solved_lead, tail_rows], axis=0)
    return reduced.reshape(rounds, strip_width, 2, row_run)


def solution(mesh):
    in_specs = (P(None, "col", None, "row"), P(None, "col", None, "row"))
    out_specs = P(None, "col", None, "row")
    return jax.shard_map(local, mesh=mesh, in_specs=in_specs, out_specs=out_specs, check_vma=False)
```

```python
import jax
import jax.numpy as jnp
from jax import lax
from jax.sharding import PartitionSpec as P

highest = lax.Precision.HIGHEST


def times_rows(coeff, right_side):
    return jnp.dot(coeff, right_side, precision=highest, preferred_element_type=jnp.float32)


def times_rows_turned(coeff, right_turned):
    return lax.dot_general(
        coeff,
        right_turned,
        (((1,), (1,)), ((), ())),
        precision=highest,
        preferred_element_type=jnp.float32,
    )


def local(strip, lower):
    rounds = strip.shape[0]
    strip_width = strip.shape[1]
    row_run = strip.shape[3]
    row_count = lax.axis_size("row")
    col_count = lax.axis_size("col")
    block_size = row_run * row_count
    cols_here = rounds * strip_width
    strip_rows = strip.reshape(cols_here, 2 * row_run)
    gathered = lax.all_gather(lower[0], "col", axis=0, tiled=True)
    first_cols = gathered[:block_size, 0, :]
    cross_cols = gathered[block_size:, 0, :]
    second_cols = gathered[block_size:, 1, :]

    col_position = lax.axis_index("col")
    lower_half = col_position * strip_width // block_size
    own_rows = lax.all_gather(lower[0], "row", axis=2, tiled=True)
    diag_rows = lax.dynamic_index_in_dim(own_rows, lower_half, 1, keepdims=False)
    below = lower_half == 1

    cross_mix = lax.all_gather(times_rows(own_rows[:, 1, :], cross_cols), "row", axis=1, tiled=True)
    chained_piece = times_rows(cross_mix, first_cols)
    chained = lax.all_gather(chained_piece, "row", axis=1, tiled=True)
    chained_cols = lax.all_gather(chained_piece, "col", axis=0, tiled=True)[block_size:]

    inverse_cols = jnp.concatenate(
        [
            jnp.concatenate([first_cols, jnp.zeros_like(first_cols)], axis=1),
            jnp.concatenate([-chained_cols, second_cols], axis=1),
        ],
        axis=0,
    )
    inverse_cols = inverse_cols.reshape(2, row_count, row_run, 2 * row_run).transpose(1, 0, 2, 3)
    inverse_cols = inverse_cols.reshape(2 * block_size, 2 * row_run)
    strip_lead = lax.all_gather(strip[0], "col", axis=0, tiled=True)
    strip_lead = strip_lead.reshape(2 * block_size, 2 * row_run)
    strip_first = strip_lead[:block_size]
    strip_diag = lax.dynamic_slice_in_dim(strip_lead, lower_half * block_size, block_size, 0)
    chained_term = jnp.where(below, times_rows(chained, strip_first), 0.0)
    mixed = times_rows(diag_rows, strip_diag) - chained_term
    solved_lead = lax.psum_scatter(
        times_rows_turned(inverse_cols, mixed), "row", scatter_dimension=0, tiled=True
    ).T
    everything = lax.all_gather(solved_lead, "col", axis=0, tiled=True)

    trail_count = cols_here - strip_width
    trail_part = lower[1:].reshape(trail_count, 2, 1, row_run)
    copies = jnp.broadcast_to(trail_part, (trail_count, 2, row_count, row_run))
    full_left = lax.all_to_all(copies, "row", split_axis=2, concat_axis=2, tiled=True)
    full_left = full_left.reshape(trail_count, 2 * block_size)
    left_update = lax.optimization_barrier(times_rows(full_left, everything))
    summed = lax.psum_scatter(
        times_rows_turned(inverse_cols, strip_rows[strip_width:]),
        "row",
        scatter_dimension=0,
        tiled=True,
    )
    tail_rows = summed.T - left_update
    reduced = jnp.concatenate([solved_lead, tail_rows], axis=0)
    return reduced.reshape(rounds, strip_width, 2, row_run)


def solution(mesh):
    in_specs = (P(None, "col", None, "row"), P(None, "col", None, "row"))
    out_specs = P(None, "col", None, "row")
    return jax.shard_map(local, mesh=mesh, in_specs=in_specs, out_specs=out_specs, check_vma=False)
```

```python
import jax
import jax.numpy as jnp
from jax import lax
from jax.sharding import PartitionSpec as P

highest = lax.Precision.HIGHEST


def times_rows(coeff, right_side):
    return jnp.dot(coeff, right_side, precision=highest, preferred_element_type=jnp.float32)


def times_rows_turned(coeff, right_turned):
    return lax.dot_general(
        coeff,
        right_turned,
        (((1,), (1,)), ((), ())),
        precision=highest,
        preferred_element_type=jnp.float32,
    )


def local(strip, lower):
    rounds = strip.shape[0]
    strip_width = strip.shape[1]
    row_run = strip.shape[3]
    row_count = lax.axis_size("row")
    col_count = lax.axis_size("col")
    block_size = row_run * row_count
    cols_here = rounds * strip_width
    strip_rows = strip.reshape(cols_here, 2 * row_run)
    gathered = lax.all_gather(lower[0], "col", axis=0, tiled=True)
    first_cols = gathered[:block_size, 0, :]
    cross_cols = gathered[block_size:, 0, :]
    second_cols = gathered[block_size:, 1, :]

    col_position = lax.axis_index("col")
    lower_half = col_position * strip_width // block_size
    own_rows = lax.all_gather(lower[0], "row", axis=2, tiled=True)
    diag_rows = lax.dynamic_index_in_dim(own_rows, lower_half, 1, keepdims=False)
    below = lower_half == 1

    cross_mix = lax.all_gather(times_rows(own_rows[:, 1, :], cross_cols), "row", axis=1, tiled=True)
    chained_piece = times_rows(cross_mix, first_cols)
    chained = lax.all_gather(chained_piece, "row", axis=1, tiled=True)
    joined = jnp.concatenate([strip[0].reshape(strip_width, 2 * row_run), chained_piece], axis=1)
    joined = lax.all_gather(joined, "col", axis=0, tiled=True)
    strip_lead = joined[:, : 2 * row_run]
    chained_cols = joined[block_size:, 2 * row_run :]

    inverse_cols = jnp.concatenate(
        [
            jnp.concatenate([first_cols, jnp.zeros_like(first_cols)], axis=1),
            jnp.concatenate([-chained_cols, second_cols], axis=1),
        ],
        axis=0,
    )
    inverse_cols = inverse_cols.reshape(2, row_count, row_run, 2 * row_run).transpose(1, 0, 2, 3)
    inverse_cols = inverse_cols.reshape(2 * block_size, 2 * row_run)
    strip_first = strip_lead[:block_size]
    strip_diag = lax.dynamic_slice_in_dim(strip_lead, lower_half * block_size, block_size, 0)
    chained_term = jnp.where(below, times_rows(chained, strip_first), 0.0)
    mixed = times_rows(diag_rows, strip_diag) - chained_term
    solved_lead = lax.psum_scatter(
        times_rows_turned(inverse_cols, mixed), "row", scatter_dimension=0, tiled=True
    ).T
    everything = lax.all_gather(solved_lead, "col", axis=0, tiled=True)

    trail_count = cols_here - strip_width
    trail_part = lower[1:].reshape(trail_count, 2, 1, row_run)
    copies = jnp.broadcast_to(trail_part, (trail_count, 2, row_count, row_run))
    full_left = lax.all_to_all(copies, "row", split_axis=2, concat_axis=2, tiled=True)
    full_left = full_left.reshape(trail_count, 2 * block_size)
    left_update = lax.optimization_barrier(times_rows(full_left, everything))
    summed = lax.psum_scatter(
        times_rows_turned(inverse_cols, strip_rows[strip_width:]),
        "row",
        scatter_dimension=0,
        tiled=True,
    )
    tail_rows = summed.T - left_update
    reduced = jnp.concatenate([solved_lead, tail_rows], axis=0)
    return reduced.reshape(rounds, strip_width, 2, row_run)


def solution(mesh):
    in_specs = (P(None, "col", None, "row"), P(None, "col", None, "row"))
    out_specs = P(None, "col", None, "row")
    return jax.shard_map(local, mesh=mesh, in_specs=in_specs, out_specs=out_specs, check_vma=False)
```

```python
import jax
import jax.numpy as jnp
from jax import lax
from jax.sharding import PartitionSpec as P

highest = lax.Precision.HIGHEST


def times_rows(coeff, right_side):
    return jnp.dot(coeff, right_side, precision=highest, preferred_element_type=jnp.float32)


def times_rows_turned(coeff, right_turned):
    return lax.dot_general(
        coeff,
        right_turned,
        (((1,), (1,)), ((), ())),
        precision=highest,
        preferred_element_type=jnp.float32,
    )


def local(strip, lower):
    rounds = strip.shape[0]
    strip_width = strip.shape[1]
    row_run = strip.shape[3]
    row_count = lax.axis_size("row")
    col_count = lax.axis_size("col")
    block_size = row_run * row_count
    cols_here = rounds * strip_width
    strip_rows = strip.reshape(cols_here, 2 * row_run)
    gathered = lax.all_gather(lower[0], "col", axis=0, tiled=True)
    first_cols = gathered[:block_size, 0, :]
    cross_cols = gathered[block_size:, 0, :]
    second_cols = gathered[block_size:, 1, :]

    col_position = lax.axis_index("col")
    lower_half = col_position * strip_width // block_size
    own_rows = lax.all_gather(lower[0], "row", axis=2, tiled=True)
    diag_rows = lax.dynamic_index_in_dim(own_rows, lower_half, 1, keepdims=False)
    below = lower_half == 1

    cross_mix = lax.all_gather(times_rows(own_rows[:, 1, :], cross_cols), "row", axis=1, tiled=True)
    chained_piece = times_rows(cross_mix, first_cols)
    chained = lax.all_gather(chained_piece, "row", axis=1, tiled=True)
    joined = jnp.concatenate([strip[0].reshape(strip_width, 2 * row_run), chained_piece], axis=1)
    joined = lax.all_gather(joined, "col", axis=0, tiled=True)
    strip_lead = joined[:, : 2 * row_run]
    chained_cols = joined[block_size:, 2 * row_run :]

    inverse_cols = jnp.concatenate(
        [
            jnp.concatenate([first_cols, jnp.zeros_like(first_cols)], axis=1),
            jnp.concatenate([-chained_cols, second_cols], axis=1),
        ],
        axis=0,
    )
    inverse_cols = inverse_cols.reshape(2, row_count, row_run, 2 * row_run).transpose(1, 0, 2, 3)
    inverse_cols = inverse_cols.reshape(2 * block_size, 2 * row_run)
    strip_first = strip_lead[:block_size]
    strip_diag = lax.dynamic_slice_in_dim(strip_lead, lower_half * block_size, block_size, 0)
    chained_term = jnp.where(below, times_rows(chained, strip_first), 0.0)
    mixed = times_rows(diag_rows, strip_diag) - chained_term
    lead_parts = times_rows_turned(inverse_cols, mixed).reshape(row_count, 2 * row_run, strip_width)
    lead_parts = lax.all_to_all(lead_parts, "row", split_axis=0, concat_axis=0, tiled=True)
    solved_lead = lead_parts.sum(axis=0).T
    everything = lax.all_gather(solved_lead, "col", axis=0, tiled=True)

    trail_count = cols_here - strip_width
    trail_part = lower[1:].reshape(trail_count, 2, 1, row_run)
    copies = jnp.broadcast_to(trail_part, (trail_count, 2, row_count, row_run))
    full_left = lax.all_to_all(copies, "row", split_axis=2, concat_axis=2, tiled=True)
    full_left = full_left.reshape(trail_count, 2 * block_size)
    left_update = lax.optimization_barrier(times_rows(full_left, everything))
    summed = lax.psum_scatter(
        times_rows_turned(inverse_cols, strip_rows[strip_width:]),
        "row",
        scatter_dimension=0,
        tiled=True,
    )
    tail_rows = summed.T - left_update
    reduced = jnp.concatenate([solved_lead, tail_rows], axis=0)
    return reduced.reshape(rounds, strip_width, 2, row_run)


def solution(mesh):
    in_specs = (P(None, "col", None, "row"), P(None, "col", None, "row"))
    out_specs = P(None, "col", None, "row")
    return jax.shard_map(local, mesh=mesh, in_specs=in_specs, out_specs=out_specs, check_vma=False)
```

```python
import jax
import jax.numpy as jnp
from jax import lax
from jax.sharding import PartitionSpec as P

highest = lax.Precision.HIGHEST


def times_rows(coeff, right_side):
    return jnp.dot(coeff, right_side, precision=highest, preferred_element_type=jnp.float32)


def times_rows_turned(coeff, right_turned):
    return lax.dot_general(
        coeff,
        right_turned,
        (((1,), (1,)), ((), ())),
        precision=highest,
        preferred_element_type=jnp.float32,
    )


def local(strip, lower):
    rounds = strip.shape[0]
    strip_width = strip.shape[1]
    row_run = strip.shape[3]
    row_count = lax.axis_size("row")
    col_count = lax.axis_size("col")
    block_size = row_run * row_count
    cols_here = rounds * strip_width
    strip_rows = strip.reshape(cols_here, 2 * row_run)
    gathered = lax.all_gather(lower[0], "col", axis=0, tiled=True)

    trail_count = cols_here - strip_width
    chunk = trail_count // 4
    bounds = [0, chunk, 2 * chunk, trail_count]
    left_chunks = []
    for lo, hi in zip(bounds[:-1], bounds[1:]):
        trail_part = lower[1:].reshape(trail_count, 2, 1, row_run)[lo:hi]
        copies = jnp.broadcast_to(trail_part, (hi - lo, 2, row_count, row_run))
        moved = lax.all_to_all(copies, "row", split_axis=2, concat_axis=2, tiled=True)
        left_chunks.append(moved.reshape(hi - lo, 2 * block_size))
    left_chunks[0], gathered = lax.optimization_barrier((left_chunks[0], gathered))
    first_cols = gathered[:block_size, 0, :]
    cross_cols = gathered[block_size:, 0, :]
    second_cols = gathered[block_size:, 1, :]

    col_position = lax.axis_index("col")
    lower_half = col_position * strip_width // block_size
    own_rows = lax.all_gather(lower[0], "row", axis=2, tiled=True)
    diag_rows = lax.dynamic_index_in_dim(own_rows, lower_half, 1, keepdims=False)
    below = lower_half == 1

    cross_mix = lax.all_gather(times_rows(own_rows[:, 1, :], cross_cols), "row", axis=1, tiled=True)
    chained_piece = times_rows(cross_mix, first_cols)
    chained = lax.all_gather(chained_piece, "row", axis=1, tiled=True)
    left_chunks[1], chained = lax.optimization_barrier((left_chunks[1], chained))
    joined = jnp.concatenate([strip[0].reshape(strip_width, 2 * row_run), chained_piece], axis=1)
    joined = lax.all_gather(joined, "col", axis=0, tiled=True)
    strip_lead = joined[:, : 2 * row_run]
    chained_cols = joined[block_size:, 2 * row_run :]

    inverse_cols = jnp.concatenate(
        [
            jnp.concatenate([first_cols, jnp.zeros_like(first_cols)], axis=1),
            jnp.concatenate([-chained_cols, second_cols], axis=1),
        ],
        axis=0,
    )
    inverse_cols = inverse_cols.reshape(2, row_count, row_run, 2 * row_run).transpose(1, 0, 2, 3)
    inverse_cols = inverse_cols.reshape(2 * block_size, 2 * row_run)
    strip_first = strip_lead[:block_size]
    strip_diag = lax.dynamic_slice_in_dim(strip_lead, lower_half * block_size, block_size, 0)
    chained_term = jnp.where(below, times_rows(chained, strip_first), 0.0)
    mixed = times_rows(diag_rows, strip_diag) - chained_term
    lead_parts = times_rows_turned(inverse_cols, mixed).reshape(row_count, 2 * row_run, strip_width)
    lead_parts = lax.all_to_all(lead_parts, "row", split_axis=0, concat_axis=0, tiled=True)
    solved_lead = lead_parts.sum(axis=0).T
    everything = lax.all_gather(solved_lead, "col", axis=0, tiled=True)

    full_left = jnp.concatenate(left_chunks, axis=0)
    left_update = lax.optimization_barrier(times_rows(full_left, everything))
    summed = lax.psum_scatter(
        times_rows_turned(inverse_cols, strip_rows[strip_width:]),
        "row",
        scatter_dimension=0,
        tiled=True,
    )
    tail_rows = summed.T - left_update
    reduced = jnp.concatenate([solved_lead, tail_rows], axis=0)
    return reduced.reshape(rounds, strip_width, 2, row_run)


def solution(mesh):
    in_specs = (P(None, "col", None, "row"), P(None, "col", None, "row"))
    out_specs = P(None, "col", None, "row")
    return jax.shard_map(local, mesh=mesh, in_specs=in_specs, out_specs=out_specs, check_vma=False)
```

```python
import jax
import jax.numpy as jnp
from jax import lax
from jax.sharding import PartitionSpec as P

highest = lax.Precision.HIGHEST


def times_rows(coeff, right_side):
    return jnp.dot(coeff, right_side, precision=highest, preferred_element_type=jnp.float32)


def times_rows_turned(coeff, right_turned):
    return lax.dot_general(
        coeff,
        right_turned,
        (((1,), (1,)), ((), ())),
        precision=highest,
        preferred_element_type=jnp.float32,
    )


def local(strip, lower):
    rounds = strip.shape[0]
    strip_width = strip.shape[1]
    row_run = strip.shape[3]
    row_count = lax.axis_size("row")
    col_count = lax.axis_size("col")
    block_size = row_run * row_count
    cols_here = rounds * strip_width
    strip_rows = strip.reshape(cols_here, 2 * row_run)
    gathered = lax.all_gather(lower[0], "col", axis=0, tiled=True)

    trail_count = cols_here - strip_width
    chunk = trail_count // 4
    bounds = [0, chunk, 2 * chunk, trail_count]
    left_chunks = []
    for lo, hi in zip(bounds[:-1], bounds[1:]):
        trail_part = lower[1:].reshape(trail_count, 2, 1, row_run)[lo:hi]
        copies = jnp.broadcast_to(trail_part, (hi - lo, 2, row_count, row_run))
        moved = lax.all_to_all(copies, "row", split_axis=2, concat_axis=2, tiled=True)
        left_chunks.append(moved.reshape(hi - lo, 2 * block_size))
    left_chunks[0], gathered = lax.optimization_barrier((left_chunks[0], gathered))
    first_cols = gathered[:block_size, 0, :]
    cross_cols = gathered[block_size:, 0, :]
    second_cols = gathered[block_size:, 1, :]

    col_position = lax.axis_index("col")
    lower_half = col_position * strip_width // block_size
    own_rows = lax.all_gather(lower[0], "row", axis=2, tiled=True)
    diag_rows = lax.dynamic_index_in_dim(own_rows, lower_half, 1, keepdims=False)
    below = lower_half == 1

    cross_piece = times_rows(own_rows[:, 1, :], cross_cols)[:, None, :]
    cross_copies = jnp.broadcast_to(cross_piece, (strip_width, row_count, row_run))
    cross_mix = lax.all_to_all(cross_copies, "row", split_axis=1, concat_axis=1, tiled=True)
    cross_mix = cross_mix.reshape(strip_width, block_size)
    chained_piece = times_rows(cross_mix, first_cols)
    chained = lax.all_gather(chained_piece, "row", axis=1, tiled=True)
    left_chunks[1], chained = lax.optimization_barrier((left_chunks[1], chained))
    joined = jnp.concatenate([strip[0].reshape(strip_width, 2 * row_run), chained_piece], axis=1)
    joined = lax.all_gather(joined, "col", axis=0, tiled=True)
    strip_lead = joined[:, : 2 * row_run]
    chained_cols = joined[block_size:, 2 * row_run :]

    inverse_cols = jnp.concatenate(
        [
            jnp.concatenate([first_cols, jnp.zeros_like(first_cols)], axis=1),
            jnp.concatenate([-chained_cols, second_cols], axis=1),
        ],
        axis=0,
    )
    inverse_cols = inverse_cols.reshape(2, row_count, row_run, 2 * row_run).transpose(1, 0, 2, 3)
    inverse_cols = inverse_cols.reshape(2 * block_size, 2 * row_run)
    strip_first = strip_lead[:block_size]
    strip_diag = lax.dynamic_slice_in_dim(strip_lead, lower_half * block_size, block_size, 0)
    chained_term = jnp.where(below, times_rows(chained, strip_first), 0.0)
    mixed = times_rows(diag_rows, strip_diag) - chained_term
    lead_parts = times_rows_turned(inverse_cols, mixed).reshape(row_count, 2 * row_run, strip_width)
    lead_parts = lax.all_to_all(lead_parts, "row", split_axis=0, concat_axis=0, tiled=True)
    solved_lead = lead_parts.sum(axis=0).T
    everything = lax.all_gather(solved_lead, "col", axis=0, tiled=True)

    full_left = jnp.concatenate(left_chunks, axis=0)
    left_update = lax.optimization_barrier(times_rows(full_left, everything))
    summed = lax.psum_scatter(
        times_rows_turned(inverse_cols, strip_rows[strip_width:]),
        "row",
        scatter_dimension=0,
        tiled=True,
    )
    tail_rows = summed.T - left_update
    reduced = jnp.concatenate([solved_lead, tail_rows], axis=0)
    return reduced.reshape(rounds, strip_width, 2, row_run)


def solution(mesh):
    in_specs = (P(None, "col", None, "row"), P(None, "col", None, "row"))
    out_specs = P(None, "col", None, "row")
    return jax.shard_map(local, mesh=mesh, in_specs=in_specs, out_specs=out_specs, check_vma=False)
```

```python
import jax
import jax.numpy as jnp
from jax import lax
from jax.sharding import PartitionSpec as P

highest = lax.Precision.HIGHEST


def times_rows(coeff, right_side):
    return jnp.dot(coeff, right_side, precision=highest, preferred_element_type=jnp.float32)


def times_rows_turned(coeff, right_turned):
    return lax.dot_general(
        coeff,
        right_turned,
        (((1,), (1,)), ((), ())),
        precision=highest,
        preferred_element_type=jnp.float32,
    )


def local(strip, lower):
    rounds = strip.shape[0]
    strip_width = strip.shape[1]
    row_run = strip.shape[3]
    row_count = lax.axis_size("row")
    col_count = lax.axis_size("col")
    block_size = row_run * row_count
    cols_here = rounds * strip_width
    strip_rows = strip.reshape(cols_here, 2 * row_run)
    gathered = lax.all_gather(lower[0], "col", axis=0, tiled=True)

    trail_count = cols_here - strip_width
    chunk = trail_count // 4
    bounds = [0, chunk, 2 * chunk, trail_count]
    left_chunks = []
    for lo, hi in zip(bounds[:-1], bounds[1:]):
        trail_part = lower[1:].reshape(trail_count, 2, 1, row_run)[lo:hi]
        copies = jnp.broadcast_to(trail_part, (hi - lo, 2, row_count, row_run))
        moved = lax.all_to_all(copies, "row", split_axis=2, concat_axis=2, tiled=True)
        left_chunks.append(moved.reshape(hi - lo, 2 * block_size))
    left_chunks[0], gathered = lax.optimization_barrier((left_chunks[0], gathered))
    first_cols = gathered[:block_size, 0, :]
    cross_cols = gathered[block_size:, 0, :]
    second_cols = gathered[block_size:, 1, :]

    col_position = lax.axis_index("col")
    lower_half = col_position * strip_width // block_size
    own_rows = lax.all_gather(lower[0], "row", axis=2, tiled=True)
    diag_rows = lax.dynamic_index_in_dim(own_rows, lower_half, 1, keepdims=False)
    below = lower_half == 1

    cross_piece = times_rows(own_rows[:, 1, :], cross_cols)[:, None, :]
    cross_copies = jnp.broadcast_to(cross_piece, (strip_width, row_count, row_run))
    cross_mix = lax.all_to_all(cross_copies, "row", split_axis=1, concat_axis=1, tiled=True)
    cross_mix = cross_mix.reshape(strip_width, block_size)
    chained_piece = times_rows(cross_mix, first_cols)
    chained_copies = jnp.broadcast_to(chained_piece[:, None, :], (strip_width, row_count, row_run))
    chained = lax.all_to_all(chained_copies, "row", split_axis=1, concat_axis=1, tiled=True)
    chained = chained.reshape(strip_width, block_size)
    left_chunks[1], chained = lax.optimization_barrier((left_chunks[1], chained))
    joined = jnp.concatenate([strip[0].reshape(strip_width, 2 * row_run), chained_piece], axis=1)
    joined = lax.all_gather(joined, "col", axis=0, tiled=True)
    strip_lead = joined[:, : 2 * row_run]
    chained_cols = joined[block_size:, 2 * row_run :]

    inverse_cols = jnp.concatenate(
        [
            jnp.concatenate([first_cols, jnp.zeros_like(first_cols)], axis=1),
            jnp.concatenate([-chained_cols, second_cols], axis=1),
        ],
        axis=0,
    )
    inverse_cols = inverse_cols.reshape(2, row_count, row_run, 2 * row_run).transpose(1, 0, 2, 3)
    inverse_cols = inverse_cols.reshape(2 * block_size, 2 * row_run)
    strip_first = strip_lead[:block_size]
    strip_diag = lax.dynamic_slice_in_dim(strip_lead, lower_half * block_size, block_size, 0)
    chained_term = jnp.where(below, times_rows(chained, strip_first), 0.0)
    mixed = times_rows(diag_rows, strip_diag) - chained_term
    lead_parts = times_rows_turned(inverse_cols, mixed).reshape(row_count, 2 * row_run, strip_width)
    lead_parts = lax.all_to_all(lead_parts, "row", split_axis=0, concat_axis=0, tiled=True)
    solved_lead = lead_parts.sum(axis=0).T
    everything = lax.all_gather(solved_lead, "col", axis=0, tiled=True)

    full_left = jnp.concatenate(left_chunks, axis=0)
    left_update = lax.optimization_barrier(times_rows(full_left, everything))
    summed = lax.psum_scatter(
        times_rows_turned(inverse_cols, strip_rows[strip_width:]),
        "row",
        scatter_dimension=0,
        tiled=True,
    )
    tail_rows = summed.T - left_update
    reduced = jnp.concatenate([solved_lead, tail_rows], axis=0)
    return reduced.reshape(rounds, strip_width, 2, row_run)


def solution(mesh):
    in_specs = (P(None, "col", None, "row"), P(None, "col", None, "row"))
    out_specs = P(None, "col", None, "row")
    return jax.shard_map(local, mesh=mesh, in_specs=in_specs, out_specs=out_specs, check_vma=False)
```

```python
import jax
import jax.numpy as jnp
from jax import lax
from jax.sharding import PartitionSpec as P

highest = lax.Precision.HIGHEST


def times_rows(coeff, right_side):
    return jnp.dot(coeff, right_side, precision=highest, preferred_element_type=jnp.float32)


def times_rows_turned(coeff, right_turned):
    return lax.dot_general(
        coeff,
        right_turned,
        (((1,), (1,)), ((), ())),
        precision=highest,
        preferred_element_type=jnp.float32,
    )


def local(strip, lower):
    rounds = strip.shape[0]
    strip_width = strip.shape[1]
    row_run = strip.shape[3]
    row_count = lax.axis_size("row")
    col_count = lax.axis_size("col")
    block_size = row_run * row_count
    cols_here = rounds * strip_width
    strip_rows = strip.reshape(cols_here, 2 * row_run)
    gathered = lax.all_gather(lower[0], "col", axis=0, tiled=True)

    trail_count = cols_here - strip_width
    chunk = trail_count // 4
    bounds = [0, chunk, 2 * chunk, 3 * chunk, trail_count]
    left_chunks = []
    for lo, hi in zip(bounds[:-1], bounds[1:]):
        trail_part = lower[1:].reshape(trail_count, 2, 1, row_run)[lo:hi]
        copies = jnp.broadcast_to(trail_part, (hi - lo, 2, row_count, row_run))
        moved = lax.all_to_all(copies, "row", split_axis=2, concat_axis=2, tiled=True)
        left_chunks.append(moved.reshape(hi - lo, 2 * block_size))
    left_chunks[0], gathered = lax.optimization_barrier((left_chunks[0], gathered))
    first_cols = gathered[:block_size, 0, :]
    cross_cols = gathered[block_size:, 0, :]
    second_cols = gathered[block_size:, 1, :]

    col_position = lax.axis_index("col")
    lower_half = col_position * strip_width // block_size
    own_rows = lax.all_gather(lower[0], "row", axis=2, tiled=True)
    diag_rows = lax.dynamic_index_in_dim(own_rows, lower_half, 1, keepdims=False)
    below = lower_half == 1

    cross_piece = times_rows(own_rows[:, 1, :], cross_cols)[:, None, :]
    cross_copies = jnp.broadcast_to(cross_piece, (strip_width, row_count, row_run))
    cross_mix = lax.all_to_all(cross_copies, "row", split_axis=1, concat_axis=1, tiled=True)
    cross_mix = cross_mix.reshape(strip_width, block_size)
    chained_piece = times_rows(cross_mix, first_cols)
    chained_copies = jnp.broadcast_to(chained_piece[:, None, :], (strip_width, row_count, row_run))
    chained = lax.all_to_all(chained_copies, "row", split_axis=1, concat_axis=1, tiled=True)
    chained = chained.reshape(strip_width, block_size)
    left_chunks[1:], chained = lax.optimization_barrier((left_chunks[1:], chained))
    joined = jnp.concatenate([strip[0].reshape(strip_width, 2 * row_run), chained_piece], axis=1)
    joined = lax.all_gather(joined, "col", axis=0, tiled=True)
    strip_lead = joined[:, : 2 * row_run]
    chained_cols = joined[block_size:, 2 * row_run :]

    inverse_cols = jnp.concatenate(
        [
            jnp.concatenate([first_cols, jnp.zeros_like(first_cols)], axis=1),
            jnp.concatenate([-chained_cols, second_cols], axis=1),
        ],
        axis=0,
    )
    inverse_cols = inverse_cols.reshape(2, row_count, row_run, 2 * row_run).transpose(1, 0, 2, 3)
    inverse_cols = inverse_cols.reshape(2 * block_size, 2 * row_run)
    strip_first = strip_lead[:block_size]
    strip_diag = lax.dynamic_slice_in_dim(strip_lead, lower_half * block_size, block_size, 0)
    chained_term = jnp.where(below, times_rows(chained, strip_first), 0.0)
    mixed = times_rows(diag_rows, strip_diag) - chained_term
    lead_parts = times_rows_turned(inverse_cols, mixed).reshape(row_count, 2 * row_run, strip_width)
    lead_parts = lax.all_to_all(lead_parts, "row", split_axis=0, concat_axis=0, tiled=True)
    solved_lead = lead_parts.sum(axis=0).T
    everything = lax.all_gather(solved_lead, "col", axis=0, tiled=True)

    full_left = jnp.concatenate(left_chunks, axis=0)
    left_update = lax.optimization_barrier(times_rows(full_left, everything))
    trail_parts = times_rows_turned(inverse_cols, strip_rows[strip_width:])
    trail_parts = trail_parts.reshape(row_count, 2 * row_run, trail_count)
    trail_parts, solved_lead = lax.optimization_barrier((trail_parts, solved_lead))
    trail_parts = lax.all_to_all(trail_parts, "row", split_axis=0, concat_axis=0, tiled=True)
    summed = trail_parts.sum(axis=0)
    tail_rows = summed.T - left_update
    reduced = jnp.concatenate([solved_lead, tail_rows], axis=0)
    return reduced.reshape(rounds, strip_width, 2, row_run)


def solution(mesh):
    in_specs = (P(None, "col", None, "row"), P(None, "col", None, "row"))
    out_specs = P(None, "col", None, "row")
    return jax.shard_map(local, mesh=mesh, in_specs=in_specs, out_specs=out_specs, check_vma=False)
```

```python
import jax
import jax.numpy as jnp
from jax import lax
from jax.sharding import PartitionSpec as P

highest = lax.Precision.HIGHEST


def times_rows(coeff, right_side):
    return jnp.dot(coeff, right_side, precision=highest, preferred_element_type=jnp.float32)


def times_rows_turned(coeff, right_turned):
    return lax.dot_general(
        coeff,
        right_turned,
        (((1,), (1,)), ((), ())),
        precision=highest,
        preferred_element_type=jnp.float32,
    )


def local(strip, lower):
    rounds = strip.shape[0]
    strip_width = strip.shape[1]
    row_run = strip.shape[3]
    row_count = lax.axis_size("row")
    col_count = lax.axis_size("col")
    block_size = row_run * row_count
    cols_here = rounds * strip_width
    strip_rows = strip.reshape(cols_here, 2 * row_run)
    gathered = lax.all_gather(lower[0], "col", axis=0, tiled=True)

    trail_count = cols_here - strip_width
    chunk = trail_count // 4
    bounds = [0, chunk, 2 * chunk, 3 * chunk, trail_count]
    left_chunks = []
    for lo, hi in zip(bounds[:-1], bounds[1:]):
        trail_part = lower[1:].reshape(trail_count, 2, 1, row_run)[lo:hi]
        copies = jnp.broadcast_to(trail_part, (hi - lo, 2, row_count, row_run))
        moved = lax.all_to_all(copies, "row", split_axis=2, concat_axis=2, tiled=True)
        left_chunks.append(moved.reshape(hi - lo, 2 * block_size))
    left_chunks[0], gathered = lax.optimization_barrier((left_chunks[0], gathered))
    first_cols = gathered[:block_size, 0, :]
    cross_cols = gathered[block_size:, 0, :]
    second_cols = gathered[block_size:, 1, :]

    col_position = lax.axis_index("col")
    lower_half = col_position * strip_width // block_size
    own_rows = lax.all_gather(lower[0], "row", axis=2, tiled=True)
    diag_rows = lax.dynamic_index_in_dim(own_rows, lower_half, 1, keepdims=False)
    below = lower_half == 1

    cross_piece = times_rows(own_rows[:, 1, :], cross_cols)[:, None, :]
    cross_copies = jnp.broadcast_to(cross_piece, (strip_width, row_count, row_run))
    cross_mix = lax.all_to_all(cross_copies, "row", split_axis=1, concat_axis=1, tiled=True)
    cross_mix = cross_mix.reshape(strip_width, block_size)
    chained_piece = times_rows(cross_mix, first_cols)
    chained_copies = jnp.broadcast_to(chained_piece[:, None, :], (strip_width, row_count, row_run))
    chained = lax.all_to_all(chained_copies, "row", split_axis=1, concat_axis=1, tiled=True)
    chained = chained.reshape(strip_width, block_size)
    joined = jnp.concatenate([strip[0].reshape(strip_width, 2 * row_run), chained_piece], axis=1)
    joined = lax.all_gather(joined, "col", axis=0, tiled=True)
    left_chunks[1:], joined = lax.optimization_barrier((left_chunks[1:], joined))
    strip_lead = joined[:, : 2 * row_run]
    chained_cols = joined[block_size:, 2 * row_run :]

    inverse_cols = jnp.concatenate(
        [
            jnp.concatenate([first_cols, jnp.zeros_like(first_cols)], axis=1),
            jnp.concatenate([-chained_cols, second_cols], axis=1),
        ],
        axis=0,
    )
    inverse_cols = inverse_cols.reshape(2, row_count, row_run, 2 * row_run).transpose(1, 0, 2, 3)
    inverse_cols = inverse_cols.reshape(2 * block_size, 2 * row_run)
    strip_first = strip_lead[:block_size]
    strip_diag = lax.dynamic_slice_in_dim(strip_lead, lower_half * block_size, block_size, 0)
    chained_term = jnp.where(below, times_rows(chained, strip_first), 0.0)
    mixed = times_rows(diag_rows, strip_diag) - chained_term
    lead_parts = times_rows_turned(inverse_cols, mixed).reshape(row_count, 2 * row_run, strip_width)
    lead_parts = lax.all_to_all(lead_parts, "row", split_axis=0, concat_axis=0, tiled=True)
    solved_lead = lead_parts.sum(axis=0).T
    everything = lax.all_gather(solved_lead, "col", axis=0, tiled=True)

    full_left = jnp.concatenate(left_chunks, axis=0)
    left_update = lax.optimization_barrier(times_rows(full_left, everything))
    trail_parts = times_rows_turned(inverse_cols, strip_rows[strip_width:])
    trail_parts = trail_parts.reshape(row_count, 2 * row_run, trail_count)
    trail_parts, solved_lead = lax.optimization_barrier((trail_parts, solved_lead))
    trail_parts = lax.all_to_all(trail_parts, "row", split_axis=0, concat_axis=0, tiled=True)
    summed = trail_parts.sum(axis=0)
    tail_rows = summed.T - left_update
    reduced = jnp.concatenate([solved_lead, tail_rows], axis=0)
    return reduced.reshape(rounds, strip_width, 2, row_run)


def solution(mesh):
    in_specs = (P(None, "col", None, "row"), P(None, "col", None, "row"))
    out_specs = P(None, "col", None, "row")
    return jax.shard_map(local, mesh=mesh, in_specs=in_specs, out_specs=out_specs, check_vma=False)
```

```python
import jax
import jax.numpy as jnp
from jax import lax
from jax.sharding import PartitionSpec as P

highest = lax.Precision.HIGHEST


def times_rows(coeff, right_side):
    return jnp.dot(coeff, right_side, precision=highest, preferred_element_type=jnp.float32)


def times_rows_turned(coeff, right_turned):
    return lax.dot_general(
        coeff,
        right_turned,
        (((1,), (1,)), ((), ())),
        precision=highest,
        preferred_element_type=jnp.float32,
    )


def local(strip, lower):
    rounds = strip.shape[0]
    strip_width = strip.shape[1]
    row_run = strip.shape[3]
    row_count = lax.axis_size("row")
    col_count = lax.axis_size("col")
    block_size = row_run * row_count
    cols_here = rounds * strip_width
    strip_rows = strip.reshape(cols_here, 2 * row_run)
    gathered = lax.all_gather(lower[0], "col", axis=0, tiled=True)

    trail_count = cols_here - strip_width
    chunk = trail_count // 4
    bounds = [0, chunk, 2 * chunk, 3 * chunk, trail_count]
    left_chunks = []
    for lo, hi in zip(bounds[:-1], bounds[1:]):
        trail_part = lower[1:].reshape(trail_count, 2, 1, row_run)[lo:hi]
        copies = jnp.broadcast_to(trail_part, (hi - lo, 2, row_count, row_run))
        moved = lax.all_to_all(copies, "row", split_axis=2, concat_axis=2, tiled=True)
        left_chunks.append(moved.reshape(hi - lo, 2 * block_size))
    left_chunks[0], gathered = lax.optimization_barrier((left_chunks[0], gathered))
    first_cols = gathered[:block_size, 0, :]
    cross_cols = gathered[block_size:, 0, :]
    second_cols = gathered[block_size:, 1, :]

    col_position = lax.axis_index("col")
    lower_half = col_position * strip_width // block_size
    own_rows = lax.all_gather(lower[0], "row", axis=2, tiled=True)
    diag_rows = lax.dynamic_index_in_dim(own_rows, lower_half, 1, keepdims=False)
    below = lower_half == 1

    cross_piece = times_rows(own_rows[:, 1, :], cross_cols)[:, None, :]
    cross_copies = jnp.broadcast_to(cross_piece, (strip_width, row_count, row_run))
    cross_mix = lax.all_to_all(cross_copies, "row", split_axis=1, concat_axis=1, tiled=True)
    cross_mix = cross_mix.reshape(strip_width, block_size)
    chained_piece = times_rows(cross_mix, first_cols)
    chained_copies = jnp.broadcast_to(chained_piece[:, None, :], (strip_width, row_count, row_run))
    chained = lax.all_to_all(chained_copies, "row", split_axis=1, concat_axis=1, tiled=True)
    chained = chained.reshape(strip_width, block_size)
    joined = jnp.concatenate([strip[0].reshape(strip_width, 2 * row_run), chained_piece], axis=1)
    joined = lax.all_gather(joined, "col", axis=0, tiled=True)
    left_chunks[1:3], joined = lax.optimization_barrier((left_chunks[1:3], joined))
    strip_lead = joined[:, : 2 * row_run]
    chained_cols = joined[block_size:, 2 * row_run :]

    inverse_cols = jnp.concatenate(
        [
            jnp.concatenate([first_cols, jnp.zeros_like(first_cols)], axis=1),
            jnp.concatenate([-chained_cols, second_cols], axis=1),
        ],
        axis=0,
    )
    inverse_cols = inverse_cols.reshape(2, row_count, row_run, 2 * row_run).transpose(1, 0, 2, 3)
    inverse_cols = inverse_cols.reshape(2 * block_size, 2 * row_run)
    strip_first = strip_lead[:block_size]
    strip_diag = lax.dynamic_slice_in_dim(strip_lead, lower_half * block_size, block_size, 0)
    chained_term = jnp.where(below, times_rows(chained, strip_first), 0.0)
    mixed = times_rows(diag_rows, strip_diag) - chained_term
    lead_parts = times_rows_turned(inverse_cols, mixed).reshape(row_count, 2 * row_run, strip_width)
    lead_parts = lax.all_to_all(lead_parts, "row", split_axis=0, concat_axis=0, tiled=True)
    solved_lead = lead_parts.sum(axis=0).T
    everything = lax.all_gather(solved_lead, "col", axis=0, tiled=True)

    full_left = jnp.concatenate(left_chunks, axis=0)
    left_update = lax.optimization_barrier(times_rows(full_left, everything))
    trail_parts = times_rows_turned(inverse_cols, strip_rows[strip_width:])
    trail_parts = trail_parts.reshape(row_count, 2 * row_run, trail_count)
    trail_parts, solved_lead = lax.optimization_barrier((trail_parts, solved_lead))
    trail_parts = lax.all_to_all(trail_parts, "row", split_axis=0, concat_axis=0, tiled=True)
    summed = trail_parts.sum(axis=0)
    tail_rows = summed.T - left_update
    reduced = jnp.concatenate([solved_lead, tail_rows], axis=0)
    return reduced.reshape(rounds, strip_width, 2, row_run)


def solution(mesh):
    in_specs = (P(None, "col", None, "row"), P(None, "col", None, "row"))
    out_specs = P(None, "col", None, "row")
    return jax.shard_map(local, mesh=mesh, in_specs=in_specs, out_specs=out_specs, check_vma=False)
```

```python
import jax
import jax.numpy as jnp
from jax import lax
from jax.sharding import PartitionSpec as P

highest = lax.Precision.HIGHEST


def times_rows(coeff, right_side):
    return jnp.dot(coeff, right_side, precision=highest, preferred_element_type=jnp.float32)


def times_rows_turned(coeff, right_turned):
    return lax.dot_general(
        coeff,
        right_turned,
        (((1,), (1,)), ((), ())),
        precision=highest,
        preferred_element_type=jnp.float32,
    )


def local(strip, lower):
    rounds = strip.shape[0]
    strip_width = strip.shape[1]
    row_run = strip.shape[3]
    row_count = lax.axis_size("row")
    col_count = lax.axis_size("col")
    block_size = row_run * row_count
    cols_here = rounds * strip_width
    strip_rows = strip.reshape(cols_here, 2 * row_run)
    gathered = lax.all_gather(lower[0], "col", axis=0, tiled=True)

    trail_count = cols_here - strip_width
    chunk = trail_count // 4
    bounds = [0, chunk, 2 * chunk, 3 * chunk, trail_count]
    left_chunks = []
    for lo, hi in zip(bounds[:-1], bounds[1:]):
        trail_part = lower[1:].reshape(trail_count, 2, 1, row_run)[lo:hi]
        copies = jnp.broadcast_to(trail_part, (hi - lo, 2, row_count, row_run))
        moved = lax.all_to_all(copies, "row", split_axis=2, concat_axis=2, tiled=True)
        left_chunks.append(moved.reshape(hi - lo, 2 * block_size))
    left_chunks[0], gathered = lax.optimization_barrier((left_chunks[0], gathered))
    first_cols = gathered[:block_size, 0, :]
    cross_cols = gathered[block_size:, 0, :]
    second_cols = gathered[block_size:, 1, :]

    col_position = lax.axis_index("col")
    lower_half = col_position * strip_width // block_size
    own_rows = lax.all_gather(lower[0], "row", axis=2, tiled=True)
    diag_rows = lax.dynamic_index_in_dim(own_rows, lower_half, 1, keepdims=False)
    below = lower_half == 1

    cross_piece = times_rows(own_rows[:, 1, :], cross_cols)[:, None, :]
    cross_copies = jnp.broadcast_to(cross_piece, (strip_width, row_count, row_run))
    cross_mix = lax.all_to_all(cross_copies, "row", split_axis=1, concat_axis=1, tiled=True)
    cross_mix = cross_mix.reshape(strip_width, block_size)
    chained_piece = times_rows(cross_mix, first_cols)
    chained_copies = jnp.broadcast_to(chained_piece[:, None, :], (strip_width, row_count, row_run))
    chained = lax.all_to_all(chained_copies, "row", split_axis=1, concat_axis=1, tiled=True)
    chained = chained.reshape(strip_width, block_size)
    left_chunks[1], chained = lax.optimization_barrier((left_chunks[1], chained))
    joined = jnp.concatenate([strip[0].reshape(strip_width, 2 * row_run), chained_piece], axis=1)
    joined = lax.all_gather(joined, "col", axis=0, tiled=True)
    left_chunks[2:], joined = lax.optimization_barrier((left_chunks[2:], joined))
    strip_lead = joined[:, : 2 * row_run]
    chained_cols = joined[block_size:, 2 * row_run :]

    inverse_cols = jnp.concatenate(
        [
            jnp.concatenate([first_cols, jnp.zeros_like(first_cols)], axis=1),
            jnp.concatenate([-chained_cols, second_cols], axis=1),
        ],
        axis=0,
    )
    inverse_cols = inverse_cols.reshape(2, row_count, row_run, 2 * row_run).transpose(1, 0, 2, 3)
    inverse_cols = inverse_cols.reshape(2 * block_size, 2 * row_run)
    strip_first = strip_lead[:block_size]
    strip_diag = lax.dynamic_slice_in_dim(strip_lead, lower_half * block_size, block_size, 0)
    chained_term = jnp.where(below, times_rows(chained, strip_first), 0.0)
    mixed = times_rows(diag_rows, strip_diag) - chained_term
    lead_parts = times_rows_turned(inverse_cols, mixed).reshape(row_count, 2 * row_run, strip_width)
    lead_parts = lax.all_to_all(lead_parts, "row", split_axis=0, concat_axis=0, tiled=True)
    solved_lead = lead_parts.sum(axis=0).T
    everything = lax.all_gather(solved_lead, "col", axis=0, tiled=True)

    full_left = jnp.concatenate(left_chunks, axis=0)
    left_update = lax.optimization_barrier(times_rows(full_left, everything))
    trail_parts = times_rows_turned(inverse_cols, strip_rows[strip_width:])
    trail_parts = trail_parts.reshape(row_count, 2 * row_run, trail_count)
    trail_parts, solved_lead = lax.optimization_barrier((trail_parts, solved_lead))
    trail_parts = lax.all_to_all(trail_parts, "row", split_axis=0, concat_axis=0, tiled=True)
    summed = trail_parts.sum(axis=0)
    tail_rows = summed.T - left_update
    reduced = jnp.concatenate([solved_lead, tail_rows], axis=0)
    return reduced.reshape(rounds, strip_width, 2, row_run)


def solution(mesh):
    in_specs = (P(None, "col", None, "row"), P(None, "col", None, "row"))
    out_specs = P(None, "col", None, "row")
    return jax.shard_map(local, mesh=mesh, in_specs=in_specs, out_specs=out_specs, check_vma=False)
```

```python
import jax
import jax.numpy as jnp
from jax import lax
from jax.sharding import PartitionSpec as P

highest = lax.Precision.HIGHEST


def times_rows(coeff, right_side):
    return jnp.dot(coeff, right_side, precision=highest, preferred_element_type=jnp.float32)


def times_rows_turned(coeff, right_turned):
    return lax.dot_general(
        coeff,
        right_turned,
        (((1,), (1,)), ((), ())),
        precision=highest,
        preferred_element_type=jnp.float32,
    )


def local(strip, lower):
    rounds = strip.shape[0]
    strip_width = strip.shape[1]
    row_run = strip.shape[3]
    row_count = lax.axis_size("row")
    col_count = lax.axis_size("col")
    block_size = row_run * row_count
    cols_here = rounds * strip_width
    strip_rows = strip.reshape(cols_here, 2 * row_run)
    gathered = lax.all_gather(lower[0], "col", axis=0, tiled=True)

    trail_count = cols_here - strip_width
    chunk = trail_count // 4
    bounds = [0, chunk, 2 * chunk, 3 * chunk, trail_count]
    left_chunks = []
    for lo, hi in zip(bounds[:-1], bounds[1:]):
        trail_part = lower[1:].reshape(trail_count, 2, 1, row_run)[lo:hi]
        copies = jnp.broadcast_to(trail_part, (hi - lo, 2, row_count, row_run))
        moved = lax.all_to_all(copies, "row", split_axis=2, concat_axis=2, tiled=True)
        left_chunks.append(moved.reshape(hi - lo, 2 * block_size))
    left_chunks[0], gathered = lax.optimization_barrier((left_chunks[0], gathered))
    first_cols = gathered[:block_size, 0, :]
    cross_cols = gathered[block_size:, 0, :]
    second_cols = gathered[block_size:, 1, :]

    col_position = lax.axis_index("col")
    lower_half = col_position * strip_width // block_size
    own_rows = lax.all_gather(lower[0], "row", axis=2, tiled=True)
    diag_rows = lax.dynamic_index_in_dim(own_rows, lower_half, 1, keepdims=False)
    below = lower_half == 1

    cross_piece = times_rows(own_rows[:, 1, :], cross_cols)[:, None, :]
    cross_copies = jnp.broadcast_to(cross_piece, (strip_width, row_count, row_run))
    cross_mix = lax.all_to_all(cross_copies, "row", split_axis=1, concat_axis=1, tiled=True)
    cross_mix = cross_mix.reshape(strip_width, block_size)
    chained_piece = times_rows(cross_mix, first_cols)
    chained_copies = jnp.broadcast_to(chained_piece[:, None, :], (strip_width, row_count, row_run))
    chained = lax.all_to_all(chained_copies, "row", split_axis=1, concat_axis=1, tiled=True)
    chained = chained.reshape(strip_width, block_size)
    joined = jnp.concatenate([strip[0].reshape(strip_width, 2 * row_run), chained_piece], axis=1)
    joined = lax.all_gather(joined, "col", axis=0, tiled=True)
    left_chunks[1:], joined = lax.optimization_barrier((left_chunks[1:], joined))
    strip_lead = joined[:, : 2 * row_run]
    chained_cols = joined[block_size:, 2 * row_run :]

    inverse_cols = jnp.concatenate(
        [
            jnp.concatenate([first_cols, jnp.zeros_like(first_cols)], axis=1),
            jnp.concatenate([-chained_cols, second_cols], axis=1),
        ],
        axis=0,
    )
    inverse_cols = inverse_cols.reshape(2, row_count, row_run, 2 * row_run).transpose(1, 0, 2, 3)
    inverse_cols = inverse_cols.reshape(2 * block_size, 2 * row_run)
    strip_first = strip_lead[:block_size]
    strip_diag = lax.dynamic_slice_in_dim(strip_lead, lower_half * block_size, block_size, 0)
    chained_term = jnp.where(below, times_rows(chained, strip_first), 0.0)
    mixed = times_rows(diag_rows, strip_diag) - chained_term
    lead_parts = times_rows_turned(inverse_cols, mixed).reshape(row_count, 2 * row_run, strip_width)
    lead_parts = lax.all_to_all(lead_parts, "row", split_axis=0, concat_axis=0, tiled=True)
    solved_lead = lead_parts.sum(axis=0).T
    everything = lax.all_gather(solved_lead, "col", axis=0, tiled=True)

    full_left = jnp.concatenate(left_chunks, axis=0)
    left_update = jnp.dot(
        full_left, everything, precision=lax.Precision.HIGH, preferred_element_type=jnp.float32
    )
    left_update = lax.optimization_barrier(left_update)
    trail_parts = times_rows_turned(inverse_cols, strip_rows[strip_width:])
    trail_parts = trail_parts.reshape(row_count, 2 * row_run, trail_count)
    trail_parts, solved_lead = lax.optimization_barrier((trail_parts, solved_lead))
    trail_parts = lax.all_to_all(trail_parts, "row", split_axis=0, concat_axis=0, tiled=True)
    summed = trail_parts.sum(axis=0)
    tail_rows = summed.T - left_update
    reduced = jnp.concatenate([solved_lead, tail_rows], axis=0)
    return reduced.reshape(rounds, strip_width, 2, row_run)


def solution(mesh):
    in_specs = (P(None, "col", None, "row"), P(None, "col", None, "row"))
    out_specs = P(None, "col", None, "row")
    return jax.shard_map(local, mesh=mesh, in_specs=in_specs, out_specs=out_specs, check_vma=False)
```

```python
import jax
import jax.numpy as jnp
from jax import lax
from jax.sharding import PartitionSpec as P

highest = lax.Precision.HIGHEST


def times_rows(coeff, right_side):
    return jnp.dot(coeff, right_side, precision=highest, preferred_element_type=jnp.float32)


def times_rows_turned(coeff, right_turned):
    return lax.dot_general(
        coeff,
        right_turned,
        (((1,), (1,)), ((), ())),
        precision=highest,
        preferred_element_type=jnp.float32,
    )


def local(strip, lower):
    rounds = strip.shape[0]
    strip_width = strip.shape[1]
    row_run = strip.shape[3]
    row_count = lax.axis_size("row")
    col_count = lax.axis_size("col")
    block_size = row_run * row_count
    cols_here = rounds * strip_width
    strip_rows = strip.reshape(cols_here, 2 * row_run)
    gathered = lax.all_gather(lower[0], "col", axis=0, tiled=True)

    trail_count = cols_here - strip_width
    chunk = trail_count // 4
    bounds = [0, chunk, 2 * chunk, 3 * chunk, trail_count]
    left_chunks = []
    for lo, hi in zip(bounds[:-1], bounds[1:]):
        trail_part = lower[1:].reshape(trail_count, 2, 1, row_run)[lo:hi]
        copies = jnp.broadcast_to(trail_part, (hi - lo, 2, row_count, row_run))
        moved = lax.all_to_all(copies, "row", split_axis=2, concat_axis=2, tiled=True)
        left_chunks.append(moved.reshape(hi - lo, 2 * block_size))
    left_chunks[:2], gathered = lax.optimization_barrier((left_chunks[:2], gathered))
    first_cols = gathered[:block_size, 0, :]
    cross_cols = gathered[block_size:, 0, :]
    second_cols = gathered[block_size:, 1, :]

    col_position = lax.axis_index("col")
    lower_half = col_position * strip_width // block_size
    own_copies = jnp.broadcast_to(lower[0][:, :, None, :], (strip_width, 2, row_count, row_run))
    own_rows = lax.all_to_all(own_copies, "row", split_axis=2, concat_axis=2, tiled=True)
    own_rows = own_rows.reshape(strip_width, 2, block_size)
    diag_rows = lax.dynamic_index_in_dim(own_rows, lower_half, 1, keepdims=False)
    below = lower_half == 1

    cross_piece = times_rows(own_rows[:, 1, :], cross_cols)[:, None, :]
    cross_copies = jnp.broadcast_to(cross_piece, (strip_width, row_count, row_run))
    cross_mix = lax.all_to_all(cross_copies, "row", split_axis=1, concat_axis=1, tiled=True)
    cross_mix = cross_mix.reshape(strip_width, block_size)
    chained_piece = times_rows(cross_mix, first_cols)
    chained_copies = jnp.broadcast_to(chained_piece[:, None, :], (strip_width, row_count, row_run))
    chained = lax.all_to_all(chained_copies, "row", split_axis=1, concat_axis=1, tiled=True)
    chained = chained.reshape(strip_width, block_size)
    joined = jnp.concatenate([strip[0].reshape(strip_width, 2 * row_run), chained_piece], axis=1)
    joined = lax.all_gather(joined, "col", axis=0, tiled=True)
    left_chunks[2:], joined = lax.optimization_barrier((left_chunks[2:], joined))
    strip_lead = joined[:, : 2 * row_run]
    chained_cols = joined[block_size:, 2 * row_run :]

    inverse_cols = jnp.concatenate(
        [
            jnp.concatenate([first_cols, jnp.zeros_like(first_cols)], axis=1),
            jnp.concatenate([-chained_cols, second_cols], axis=1),
        ],
        axis=0,
    )
    inverse_cols = inverse_cols.reshape(2, row_count, row_run, 2 * row_run).transpose(1, 0, 2, 3)
    inverse_cols = inverse_cols.reshape(2 * block_size, 2 * row_run)
    strip_first = strip_lead[:block_size]
    strip_diag = lax.dynamic_slice_in_dim(strip_lead, lower_half * block_size, block_size, 0)
    chained_term = jnp.where(below, times_rows(chained, strip_first), 0.0)
    mixed = times_rows(diag_rows, strip_diag) - chained_term
    lead_parts = times_rows_turned(inverse_cols, mixed).reshape(row_count, 2 * row_run, strip_width)
    lead_parts = lax.all_to_all(lead_parts, "row", split_axis=0, concat_axis=0, tiled=True)
    solved_lead = lead_parts.sum(axis=0).T
    everything = lax.all_gather(solved_lead, "col", axis=0, tiled=True)

    full_left = jnp.concatenate(left_chunks, axis=0)
    left_update = lax.optimization_barrier(times_rows(full_left, everything))
    trail_parts = times_rows_turned(inverse_cols, strip_rows[strip_width:])
    trail_parts = trail_parts.reshape(row_count, 2 * row_run, trail_count)
    trail_parts, solved_lead = lax.optimization_barrier((trail_parts, solved_lead))
    trail_parts = lax.all_to_all(trail_parts, "row", split_axis=0, concat_axis=0, tiled=True)
    summed = trail_parts.sum(axis=0)
    tail_rows = summed.T - left_update
    reduced = jnp.concatenate([solved_lead, tail_rows], axis=0)
    return reduced.reshape(rounds, strip_width, 2, row_run)


def solution(mesh):
    in_specs = (P(None, "col", None, "row"), P(None, "col", None, "row"))
    out_specs = P(None, "col", None, "row")
    return jax.shard_map(local, mesh=mesh, in_specs=in_specs, out_specs=out_specs, check_vma=False)
```

```python
import jax
import jax.numpy as jnp
from jax import lax
from jax.sharding import PartitionSpec as P

highest = lax.Precision.HIGHEST


def times_rows(coeff, right_side):
    return jnp.dot(coeff, right_side, precision=highest, preferred_element_type=jnp.float32)


def times_rows_turned(coeff, right_turned):
    return lax.dot_general(
        coeff,
        right_turned,
        (((1,), (1,)), ((), ())),
        precision=highest,
        preferred_element_type=jnp.float32,
    )


def local(strip, lower):
    rounds = strip.shape[0]
    strip_width = strip.shape[1]
    row_run = strip.shape[3]
    row_count = lax.axis_size("row")
    col_count = lax.axis_size("col")
    block_size = row_run * row_count
    cols_here = rounds * strip_width
    strip_rows = strip.reshape(cols_here, 2 * row_run)
    gathered = lax.all_gather(lower[0], "col", axis=0, tiled=True)

    trail_count = cols_here - strip_width
    chunk = trail_count // 4
    bounds = [0, chunk, trail_count]
    left_chunks = []
    for lo, hi in zip(bounds[:-1], bounds[1:]):
        trail_part = lower[1:].reshape(trail_count, 2, 1, row_run)[lo:hi]
        copies = jnp.broadcast_to(trail_part, (hi - lo, 2, row_count, row_run))
        moved = lax.all_to_all(copies, "row", split_axis=2, concat_axis=2, tiled=True)
        left_chunks.append(moved.reshape(hi - lo, 2 * block_size))
    left_chunks[0], gathered = lax.optimization_barrier((left_chunks[0], gathered))
    first_cols = gathered[:block_size, 0, :]
    cross_cols = gathered[block_size:, 0, :]
    second_cols = gathered[block_size:, 1, :]

    col_position = lax.axis_index("col")
    lower_half = col_position * strip_width // block_size
    own_rows = lax.all_gather(lower[0], "row", axis=2, tiled=True)
    diag_rows = lax.dynamic_index_in_dim(own_rows, lower_half, 1, keepdims=False)
    below = lower_half == 1

    cross_piece = times_rows(own_rows[:, 1, :], cross_cols)[:, None, :]
    cross_copies = jnp.broadcast_to(cross_piece, (strip_width, row_count, row_run))
    cross_mix = lax.all_to_all(cross_copies, "row", split_axis=1, concat_axis=1, tiled=True)
    cross_mix = cross_mix.reshape(strip_width, block_size)
    chained_piece = times_rows(cross_mix, first_cols)
    chained_copies = jnp.broadcast_to(chained_piece[:, None, :], (strip_width, row_count, row_run))
    chained = lax.all_to_all(chained_copies, "row", split_axis=1, concat_axis=1, tiled=True)
    chained = chained.reshape(strip_width, block_size)
    joined = jnp.concatenate([strip[0].reshape(strip_width, 2 * row_run), chained_piece], axis=1)
    joined = lax.all_gather(joined, "col", axis=0, tiled=True)
    left_chunks[1:], joined = lax.optimization_barrier((left_chunks[1:], joined))
    strip_lead = joined[:, : 2 * row_run]
    chained_cols = joined[block_size:, 2 * row_run :]

    inverse_cols = jnp.concatenate(
        [
            jnp.concatenate([first_cols, jnp.zeros_like(first_cols)], axis=1),
            jnp.concatenate([-chained_cols, second_cols], axis=1),
        ],
        axis=0,
    )
    inverse_cols = inverse_cols.reshape(2, row_count, row_run, 2 * row_run).transpose(1, 0, 2, 3)
    inverse_cols = inverse_cols.reshape(2 * block_size, 2 * row_run)
    strip_first = strip_lead[:block_size]
    strip_diag = lax.dynamic_slice_in_dim(strip_lead, lower_half * block_size, block_size, 0)
    chained_term = jnp.where(below, times_rows(chained, strip_first), 0.0)
    mixed = times_rows(diag_rows, strip_diag) - chained_term
    lead_parts = times_rows_turned(inverse_cols, mixed).reshape(row_count, 2 * row_run, strip_width)
    lead_parts = lax.all_to_all(lead_parts, "row", split_axis=0, concat_axis=0, tiled=True)
    solved_lead = lead_parts.sum(axis=0).T
    everything = lax.all_gather(solved_lead, "col", axis=0, tiled=True)

    full_left = jnp.concatenate(left_chunks, axis=0)
    left_update = lax.optimization_barrier(times_rows(full_left, everything))
    trail_parts = times_rows_turned(inverse_cols, strip_rows[strip_width:])
    trail_parts = trail_parts.reshape(row_count, 2 * row_run, trail_count)
    trail_parts, solved_lead = lax.optimization_barrier((trail_parts, solved_lead))
    trail_parts = lax.all_to_all(trail_parts, "row", split_axis=0, concat_axis=0, tiled=True)
    summed = trail_parts.sum(axis=0)
    tail_rows = summed.T - left_update
    reduced = jnp.concatenate([solved_lead, tail_rows], axis=0)
    return reduced.reshape(rounds, strip_width, 2, row_run)


def solution(mesh):
    in_specs = (P(None, "col", None, "row"), P(None, "col", None, "row"))
    out_specs = P(None, "col", None, "row")
    return jax.shard_map(local, mesh=mesh, in_specs=in_specs, out_specs=out_specs, check_vma=False)
```

```python
import jax
import jax.numpy as jnp
from jax import lax
from jax.sharding import PartitionSpec as P

highest = lax.Precision.HIGHEST


def times_rows(coeff, right_side):
    return jnp.dot(coeff, right_side, precision=highest, preferred_element_type=jnp.float32)


def times_rows_turned(coeff, right_turned):
    return lax.dot_general(
        coeff,
        right_turned,
        (((1,), (1,)), ((), ())),
        precision=highest,
        preferred_element_type=jnp.float32,
    )


def local(strip, lower):
    rounds = strip.shape[0]
    strip_width = strip.shape[1]
    row_run = strip.shape[3]
    row_count = lax.axis_size("row")
    col_count = lax.axis_size("col")
    block_size = row_run * row_count
    cols_here = rounds * strip_width
    strip_rows = strip.reshape(cols_here, 2 * row_run)
    gathered = lax.all_gather(lower[0], "col", axis=0, tiled=True)

    trail_count = cols_here - strip_width
    chunk = trail_count // 8
    bounds = [index * chunk for index in range(8)] + [trail_count]
    left_chunks = []
    for lo, hi in zip(bounds[:-1], bounds[1:]):
        trail_part = lower[1:].reshape(trail_count, 2, 1, row_run)[lo:hi]
        copies = jnp.broadcast_to(trail_part, (hi - lo, 2, row_count, row_run))
        moved = lax.all_to_all(copies, "row", split_axis=2, concat_axis=2, tiled=True)
        left_chunks.append(moved.reshape(hi - lo, 2 * block_size))
    left_chunks[0], gathered = lax.optimization_barrier((left_chunks[0], gathered))
    first_cols = gathered[:block_size, 0, :]
    cross_cols = gathered[block_size:, 0, :]
    second_cols = gathered[block_size:, 1, :]

    col_position = lax.axis_index("col")
    lower_half = col_position * strip_width // block_size
    own_rows = lax.all_gather(lower[0], "row", axis=2, tiled=True)
    diag_rows = lax.dynamic_index_in_dim(own_rows, lower_half, 1, keepdims=False)
    below = lower_half == 1

    cross_piece = times_rows(own_rows[:, 1, :], cross_cols)[:, None, :]
    cross_copies = jnp.broadcast_to(cross_piece, (strip_width, row_count, row_run))
    cross_mix = lax.all_to_all(cross_copies, "row", split_axis=1, concat_axis=1, tiled=True)
    cross_mix = cross_mix.reshape(strip_width, block_size)
    chained_piece = times_rows(cross_mix, first_cols)
    chained_copies = jnp.broadcast_to(chained_piece[:, None, :], (strip_width, row_count, row_run))
    chained = lax.all_to_all(chained_copies, "row", split_axis=1, concat_axis=1, tiled=True)
    chained = chained.reshape(strip_width, block_size)
    joined = jnp.concatenate([strip[0].reshape(strip_width, 2 * row_run), chained_piece], axis=1)
    joined = lax.all_gather(joined, "col", axis=0, tiled=True)
    left_chunks[1:], joined = lax.optimization_barrier((left_chunks[1:], joined))
    strip_lead = joined[:, : 2 * row_run]
    chained_cols = joined[block_size:, 2 * row_run :]

    inverse_cols = jnp.concatenate(
        [
            jnp.concatenate([first_cols, jnp.zeros_like(first_cols)], axis=1),
            jnp.concatenate([-chained_cols, second_cols], axis=1),
        ],
        axis=0,
    )
    inverse_cols = inverse_cols.reshape(2, row_count, row_run, 2 * row_run).transpose(1, 0, 2, 3)
    inverse_cols = inverse_cols.reshape(2 * block_size, 2 * row_run)
    strip_first = strip_lead[:block_size]
    strip_diag = lax.dynamic_slice_in_dim(strip_lead, lower_half * block_size, block_size, 0)
    chained_term = jnp.where(below, times_rows(chained, strip_first), 0.0)
    mixed = times_rows(diag_rows, strip_diag) - chained_term
    lead_parts = times_rows_turned(inverse_cols, mixed).reshape(row_count, 2 * row_run, strip_width)
    lead_parts = lax.all_to_all(lead_parts, "row", split_axis=0, concat_axis=0, tiled=True)
    solved_lead = lead_parts.sum(axis=0).T
    everything = lax.all_gather(solved_lead, "col", axis=0, tiled=True)

    full_left = jnp.concatenate(left_chunks, axis=0)
    left_update = lax.optimization_barrier(times_rows(full_left, everything))
    trail_parts = times_rows_turned(inverse_cols, strip_rows[strip_width:])
    trail_parts = trail_parts.reshape(row_count, 2 * row_run, trail_count)
    trail_parts, solved_lead = lax.optimization_barrier((trail_parts, solved_lead))
    trail_parts = lax.all_to_all(trail_parts, "row", split_axis=0, concat_axis=0, tiled=True)
    summed = trail_parts.sum(axis=0)
    tail_rows = summed.T - left_update
    reduced = jnp.concatenate([solved_lead, tail_rows], axis=0)
    return reduced.reshape(rounds, strip_width, 2, row_run)


def solution(mesh):
    in_specs = (P(None, "col", None, "row"), P(None, "col", None, "row"))
    out_specs = P(None, "col", None, "row")
    return jax.shard_map(local, mesh=mesh, in_specs=in_specs, out_specs=out_specs, check_vma=False)
```

```python
import jax
import jax.numpy as jnp
from jax import lax
from jax.sharding import PartitionSpec as P

highest = lax.Precision.HIGHEST


def times_rows(coeff, right_side):
    return jnp.dot(coeff, right_side, precision=highest, preferred_element_type=jnp.float32)


def times_rows_turned(coeff, right_turned):
    return lax.dot_general(
        coeff,
        right_turned,
        (((1,), (1,)), ((), ())),
        precision=highest,
        preferred_element_type=jnp.float32,
    )


def local(strip, lower):
    rounds = strip.shape[0]
    strip_width = strip.shape[1]
    row_run = strip.shape[3]
    row_count = lax.axis_size("row")
    col_count = lax.axis_size("col")
    block_size = row_run * row_count
    cols_here = rounds * strip_width
    strip_rows = strip.reshape(cols_here, 2 * row_run)
    gathered = lax.all_gather(lower[0], "col", axis=0, tiled=True)

    trail_count = cols_here - strip_width
    chunk = trail_count // 8
    bounds = [0, 3 * chunk, 5 * chunk, 7 * chunk, trail_count]
    left_chunks = []
    for lo, hi in zip(bounds[:-1], bounds[1:]):
        trail_part = lower[1:].reshape(trail_count, 2, 1, row_run)[lo:hi]
        copies = jnp.broadcast_to(trail_part, (hi - lo, 2, row_count, row_run))
        moved = lax.all_to_all(copies, "row", split_axis=2, concat_axis=2, tiled=True)
        left_chunks.append(moved.reshape(hi - lo, 2 * block_size))
    left_chunks[0], gathered = lax.optimization_barrier((left_chunks[0], gathered))
    first_cols = gathered[:block_size, 0, :]
    cross_cols = gathered[block_size:, 0, :]
    second_cols = gathered[block_size:, 1, :]

    col_position = lax.axis_index("col")
    lower_half = col_position * strip_width // block_size
    own_rows = lax.all_gather(lower[0], "row", axis=2, tiled=True)
    diag_rows = lax.dynamic_index_in_dim(own_rows, lower_half, 1, keepdims=False)
    below = lower_half == 1

    cross_piece = times_rows(own_rows[:, 1, :], cross_cols)[:, None, :]
    cross_copies = jnp.broadcast_to(cross_piece, (strip_width, row_count, row_run))
    cross_mix = lax.all_to_all(cross_copies, "row", split_axis=1, concat_axis=1, tiled=True)
    cross_mix = cross_mix.reshape(strip_width, block_size)
    chained_piece = times_rows(cross_mix, first_cols)
    chained_copies = jnp.broadcast_to(chained_piece[:, None, :], (strip_width, row_count, row_run))
    chained = lax.all_to_all(chained_copies, "row", split_axis=1, concat_axis=1, tiled=True)
    chained = chained.reshape(strip_width, block_size)
    joined = jnp.concatenate([strip[0].reshape(strip_width, 2 * row_run), chained_piece], axis=1)
    joined = lax.all_gather(joined, "col", axis=0, tiled=True)
    left_chunks[1:], joined = lax.optimization_barrier((left_chunks[1:], joined))
    strip_lead = joined[:, : 2 * row_run]
    chained_cols = joined[block_size:, 2 * row_run :]

    inverse_cols = jnp.concatenate(
        [
            jnp.concatenate([first_cols, jnp.zeros_like(first_cols)], axis=1),
            jnp.concatenate([-chained_cols, second_cols], axis=1),
        ],
        axis=0,
    )
    inverse_cols = inverse_cols.reshape(2, row_count, row_run, 2 * row_run).transpose(1, 0, 2, 3)
    inverse_cols = inverse_cols.reshape(2 * block_size, 2 * row_run)
    strip_first = strip_lead[:block_size]
    strip_diag = lax.dynamic_slice_in_dim(strip_lead, lower_half * block_size, block_size, 0)
    chained_term = jnp.where(below, times_rows(chained, strip_first), 0.0)
    mixed = times_rows(diag_rows, strip_diag) - chained_term
    lead_parts = times_rows_turned(inverse_cols, mixed).reshape(row_count, 2 * row_run, strip_width)
    lead_parts = lax.all_to_all(lead_parts, "row", split_axis=0, concat_axis=0, tiled=True)
    solved_lead = lead_parts.sum(axis=0).T
    everything = lax.all_gather(solved_lead, "col", axis=0, tiled=True)

    full_left = jnp.concatenate(left_chunks, axis=0)
    left_update = lax.optimization_barrier(times_rows(full_left, everything))
    trail_parts = times_rows_turned(inverse_cols, strip_rows[strip_width:])
    trail_parts = trail_parts.reshape(row_count, 2 * row_run, trail_count)
    trail_parts, solved_lead = lax.optimization_barrier((trail_parts, solved_lead))
    trail_parts = lax.all_to_all(trail_parts, "row", split_axis=0, concat_axis=0, tiled=True)
    summed = trail_parts.sum(axis=0)
    tail_rows = summed.T - left_update
    reduced = jnp.concatenate([solved_lead, tail_rows], axis=0)
    return reduced.reshape(rounds, strip_width, 2, row_run)


def solution(mesh):
    in_specs = (P(None, "col", None, "row"), P(None, "col", None, "row"))
    out_specs = P(None, "col", None, "row")
    return jax.shard_map(local, mesh=mesh, in_specs=in_specs, out_specs=out_specs, check_vma=False)
```
